256 devices in a mesh: dp: 16 (over z, core), help: 16 (over y, x).
Axes of the slice: x: 4, y: 4, z: 8, core: 2. Of those that a mesh axis runs over, the one named last changes fastest.
Arguments:
- queries: bfloat16 [65536, 16, 128], P(('dp', 'help')), may hold values from -48 to 48
- keys_values: bfloat16 [65536, 4, 256], P(('dp', 'help')), may hold values from -4 to 4
- segment_ids: int32 [16, 4096], P('dp', 'help'), may hold values from 0 to 3, never falling along the last dimension, each value on 1 to 2048 neighbouring positions
- residual: bfloat16 [65536, 4096], P(('dp', 'help')), may hold values from -3 to 3
- out_weight: bfloat16 [2048, 4096], P(None, 'dp'), may hold values from -1 to 1
Outputs:
- layer_out: bfloat16 [65536, 4096], P(('dp', 'help'))
The draws below stay inside these ranges and needn't reach their ends.
All inputs are finite; a program needn't handle non-finite values.
Results may differ from the reference program's by a relative error of at most 0.0085.
Values may be sent and summed in bfloat16 or wider, within the bound.
No kernel may reach another device: no remote copies, remote signals or barrier semaphores. Data moves between devices by JAX's collectives and lax.ppermute only.
A program may use at most 128 MiB of HBM per device.

```python
import math
import jax
import jax.numpy as jnp
import numpy as np
from jax import lax

D = 4096
HEAD_DIM = 128
HEADS = 16
KV_HEADS = 4
COUNT = 4
ROW = 4096
MOST = 2048
ROWS = 16
TOKENS = 65536


def paired_draw(key):
    base = jax.random.fold_in(key, 911)
    key_query, key_pairs = jax.random.split(base, 2)
    queries = jnp.clip(jax.random.normal(key_query, (TOKENS, HEADS, HEAD_DIM), jnp.float32), -4.0, 4.0)
    pairs = jnp.clip(jax.random.normal(key_pairs, (TOKENS, KV_HEADS, 2 * HEAD_DIM), jnp.float32), -4.0, 4.0)
    return (queries, pairs)


def draw_queries(key, part):
    return paired_draw(key)[0].astype(jnp.bfloat16)


def draw_keys_values(key, part):
    return paired_draw(key)[1].astype(jnp.bfloat16)


def block_levels(rng, extent, pieces, smallest, high):
    loudness = 1.0
    for position, parts in pieces:
        steps = jax.random.uniform(jax.random.fold_in(jax.random.fold_in(rng, 6), position), (parts,), jnp.float32, smallest / len(pieces), high / len(pieces))
        loudness = loudness * jnp.repeat(jnp.exp(steps), extent[position] // parts).reshape((-1,) + (1,) * (len(extent) - 1 - position))
    return loudness


def profile(amount, total, most, slope):
    loads = [(1 << 20) // math.isqrt(rank ** slope) + 1 for rank in range(2, amount + 1)]
    surplus, counts = total - most - (amount - 1), [1] * (amount - 1)
    while surplus > 0:
        candidates = [i for i in range(amount - 1) if counts[i] < most]
        mass, remaining = sum([loads[i] for i in candidates]), surplus
        for i in candidates:
            addition = min(most - counts[i], max(1, remaining * loads[i] // mass), surplus)
            counts[i] = counts[i] + addition
            surplus = surplus - addition
    return np.array([most] + counts)


def uneven(own_key, number_of, total, reach, lean):
    if number_of == 2:
        one = jax.random.randint(own_key, (), max(1, total - reach), min(reach, total - 1) + 1)
        return jnp.stack([one, total - one])
    tallies = jnp.asarray(profile(number_of, total, reach, lean), jnp.int32)
    twos = (number_of - 1) // 2
    giver, receiver = tallies[1:1 + 2 * twos:2], tallies[2:2 + 2 * twos:2]
    room = jnp.minimum(giver - 1, reach - receiver)
    passed = jax.random.randint(jax.random.fold_in(own_key, 1), (twos,), 0, 1 << 20) % (room + 1)
    tallies = tallies.at[1:1 + 2 * twos:2].set(giver - passed).at[2:2 + 2 * twos:2].set(receiver + passed)
    return tallies[jax.random.permutation(jax.random.fold_in(own_key, 2), number_of)]


def gaussian(rng, shape, spread, most, cuts=(), kind=jnp.bfloat16):
    values = spread * jax.random.normal(rng, shape, jnp.float32)
    if cuts:
        values = values * block_levels(rng, shape, cuts, -0.22, 0.18)
    return jnp.clip(values, -most, most).astype(kind)


def setup_inputs(seed: int = 0) -> dict:
    arg_keys = jax.random.split(jax.random.key(seed), 6)
    return {
        "queries": draw_queries(jax.random.fold_in(arg_keys[5], 71), 0),
        "keys_values": draw_keys_values(jax.random.fold_in(arg_keys[5], 71), 0),
        "segment_ids": jax.vmap(lambda own: jnp.searchsorted(jnp.cumsum(uneven(own, COUNT, ROW, MOST, 2)), jnp.arange(ROW), side="right"))(jax.random.split(arg_keys[2], ROWS)).reshape((ROWS, ROW)).astype(jnp.int32),
        "residual": gaussian(arg_keys[3], (TOKENS, D), 0.5, 3.0, ((0, 256),)),
        "out_weight": gaussian(arg_keys[4], (HEADS * HEAD_DIM, D), (HEADS * HEAD_DIM // 64) ** -0.5, 1.0, ((1, 16),)),
    }


masked_score = -1e+30

def reference(queries, keys_values, segment_ids, residual, out_weight):
    group_size = HEADS // KV_HEADS
    score_scale = 1.0 / math.sqrt(HEAD_DIM)
    block_rows = min(512, ROW)
    window = min(MOST + block_rows, ROW)
    query_blocks = ROW // block_rows
    row_queries = queries.reshape(ROWS, ROW, HEADS, HEAD_DIM)
    row_keys = keys_values.reshape(ROWS, ROW, KV_HEADS, 2 * HEAD_DIM)
    row_stream = residual.reshape(ROWS, ROW, D)

    def one_row(row_inputs):
        row_q, row_kv, row_seg, row_res = row_inputs

        def one_block(block_index):
            query_start = (block_index * block_rows).astype(jnp.int32)
            key_start = jnp.clip(query_start + block_rows - window, 0, ROW - window).astype(jnp.int32)
            block_q = lax.dynamic_slice_in_dim(row_q, query_start, block_rows, 0)
            block_q = block_q.reshape(block_rows, KV_HEADS, group_size, HEAD_DIM).astype(jnp.float32)
            block_kv = lax.dynamic_slice_in_dim(row_kv, key_start, window, 0).astype(jnp.float32)
            keys = block_kv[..., :HEAD_DIM]
            values = block_kv[..., HEAD_DIM:]
            query_pos = query_start + jnp.arange(block_rows, dtype=jnp.int32)
            key_pos = key_start + jnp.arange(window, dtype=jnp.int32)
            query_seg = lax.dynamic_slice_in_dim(row_seg, query_start, block_rows, 0)
            key_seg = lax.dynamic_slice_in_dim(row_seg, key_start, window, 0)
            allowed = (key_pos[None, :] <= query_pos[:, None]) & (key_seg[None, :] == query_seg[:, None])
            scores = jnp.einsum('qhgd,thd->hgqt', block_q, keys) * score_scale
            scores = jnp.where(allowed, scores, masked_score)
            maxima = lax.optimization_barrier(jnp.max(scores, axis=-1, keepdims=True))
            weights = jnp.where(allowed, jnp.exp(scores - maxima), 0.0)
            totals = lax.optimization_barrier(jnp.sum(weights, axis=-1))
            rounded = lax.optimization_barrier(weights.astype(jnp.bfloat16)).astype(jnp.float32)
            mixed = jnp.einsum('hgqt,thd->qhgd', rounded, values)
            result = mixed / jnp.transpose(totals, (2, 0, 1))[..., None]
            return result.astype(jnp.bfloat16).reshape(block_rows, HEADS * HEAD_DIM)
        attended = lax.map(one_block, jnp.arange(query_blocks, dtype=jnp.int32)).reshape(ROW, HEADS * HEAD_DIM)
        projected = jnp.dot(attended, out_weight, preferred_element_type=jnp.float32)
        return (row_res.astype(jnp.float32) + projected).astype(jnp.bfloat16)
    layer_out = lax.map(one_row, (row_queries, row_keys, segment_ids, row_stream))
    return layer_out.reshape(TOKENS, D)
```

```python
import math

import jax
import jax.numpy as jnp
from jax import lax
from jax.sharding import Mesh
from jax.sharding import PartitionSpec as P

masked_score = -1e30
MOST = 2048


def attend_block(
    states, block_queries, block_vals, key_pos, key_seg, query_pos, query_seg, score_scale
):
    maxima, totals, running = states
    head_dim = block_queries.shape[-1]
    keys = block_vals[..., :head_dim]
    values = block_vals[..., head_dim:]
    scores = (
        jnp.einsum("qhgd,thd->hgqt", block_queries, keys, preferred_element_type=jnp.float32)
        * score_scale
    )
    allowed = (key_pos[None, :] <= query_pos[:, None]) & (key_seg[None, :] == query_seg[:, None])
    scores = jnp.where(allowed, scores, masked_score)
    new_max = jnp.maximum(maxima, jnp.max(scores, axis=-1))
    weights = jnp.where(allowed, jnp.exp(scores - new_max[..., None]), 0.0)
    factor = jnp.exp(maxima - new_max)
    totals = totals * factor + jnp.sum(weights, axis=-1)
    mixed = jnp.einsum(
        "hgqt,thd->qhgd", weights.astype(jnp.bfloat16), values, preferred_element_type=jnp.float32
    )
    running = running * jnp.transpose(factor, (2, 0, 1))[..., None] + mixed
    return (new_max, totals, running)


def start_state(rows_count, heads_kv, group_size, head_dim):
    maxima = jnp.full((heads_kv, group_size, rows_count), masked_score, jnp.float32)
    totals = jnp.zeros((heads_kv, group_size, rows_count), jnp.float32)
    running = jnp.zeros((rows_count, heads_kv, group_size, head_dim), jnp.float32)
    return (maxima, totals, running)


def finish(states):
    maxima, totals, running = states
    return (running / jnp.transpose(totals, (2, 0, 1))[..., None]).astype(jnp.bfloat16)


def tokens_attention(queries, keys_values, seg_local, helper, help_size):
    local_rows, heads, head_dim = queries.shape
    heads_kv = keys_values.shape[1]
    group_size = heads // heads_kv
    score_scale = 1.0 / math.sqrt(head_dim)
    query_pos = helper * local_rows + jnp.arange(local_rows, dtype=jnp.int32)
    grouped = queries.reshape(local_rows, heads_kv, group_size, head_dim)
    first_seg = seg_local[0]
    reach = min((MOST - 1 + local_rows - 1) // local_rows, help_size - 1)
    blocks = [(0, keys_values, seg_local)]
    for shift in range(1, reach + 1):
        pairs = [(j, j + shift) for j in range(help_size - shift)]
        blocks.append(
            (
                shift,
                lax.ppermute(keys_values, "help", pairs),
                lax.ppermute(seg_local, "help", pairs),
            )
        )
    states = start_state(local_rows, heads_kv, group_size, head_dim)
    for shift, block_vals, block_seg in blocks:
        key_pos = (helper - shift) * local_rows + jnp.arange(local_rows, dtype=jnp.int32)

        def compute(current, block_vals=block_vals, block_seg=block_seg, key_pos=key_pos):
            return attend_block(
                current, grouped, block_vals, key_pos, block_seg, query_pos, seg_local, score_scale
            )

        if shift == 0:
            states = compute(states)
        else:
            needed = jnp.logical_and(helper >= shift, block_seg[-1] >= first_seg)
            states = lax.cond(needed, compute, lambda current: current, states)
    return finish(states).reshape(local_rows, heads * head_dim)


def make_on_device(help_size):
    partner = [(0, 1), (1, 0)]

    def on_device(queries, keys_values, segment_ids, residual, out_weight):
        local_rows = queries.shape[0]
        width = out_weight.shape[1]
        gathered = lax.all_gather(out_weight, "z", axis=0)
        seg_local = segment_ids.reshape(local_rows)
        helper = lax.axis_index("help")
        core = lax.axis_index("core")
        first = core == 0
        planes = gathered.shape[0]
        stream = residual.reshape(local_rows, planes, 2, width)
        own_cols = jnp.where(first, stream[:, :, 0], stream[:, :, 1])
        other_cols = jnp.where(first, stream[:, :, 1], stream[:, :, 0])
        partner_res = lax.ppermute(other_cols, "core", partner)
        attended = tokens_attention(queries, keys_values, seg_local, helper, help_size)
        partner_att = lax.ppermute(attended, "core", partner)

        def project(rows, res):
            summed = jnp.einsum(
                "qk,zkn->qzn", rows, gathered, preferred_element_type=jnp.float32
            )
            return (res.astype(jnp.float32) + summed).astype(jnp.bfloat16)

        mine = project(attended, own_cols)
        theirs = project(partner_att, partner_res)
        back = lax.ppermute(theirs, "core", partner)
        col0 = jnp.where(first, mine, back)
        col1 = jnp.where(first, back, mine)
        return jnp.stack([col0, col1], axis=2).reshape(local_rows, planes * 2 * width)

    return on_device


def solution(mesh):
    dp_size, help_size = mesh.devices.shape
    split = Mesh(mesh.devices.reshape(dp_size // 2, 2, help_size), ("z", "core", "help"))
    rows = ("z", "core", "help")
    return jax.shard_map(
        make_on_device(help_size),
        mesh=split,
        in_specs=(
            P(rows, None, None),
            P(rows, None, None),
            P(("z", "core"), "help"),
            P(rows, None),
            P(None, ("z", "core")),
        ),
        out_specs=P(rows, None),
        check_vma=False,
    )
```

```python
import functools
import math

import jax
import jax.numpy as jnp
from jax import lax
from jax.experimental import pallas as pl
from jax.experimental.pallas import tpu as pltpu
from jax.sharding import Mesh
from jax.sharding import PartitionSpec as P

masked_score = -1e30
MOST = 2048
SEG_ROWS = 16
INTERPRET = False


def attention_kernel(
    flags_ref, q_ref, segq_ref, segk_ref, *refs, blocks, group_size, head_dim, score_scale
):
    kv_refs = refs[:blocks]
    o_ref = refs[blocks]
    m_ref, l_ref, acc_ref = refs[blocks + 1 :]
    rows = q_ref.shape[0]
    q = q_ref[...]
    stacked = jnp.concatenate(
        [q[:, h * head_dim : (h + 1) * head_dim] for h in range(group_size)], axis=0
    )
    segq = segq_ref[...]
    m_ref[...] = jnp.full(m_ref.shape, masked_score, jnp.float32)
    l_ref[...] = jnp.zeros(l_ref.shape, jnp.float32)
    acc_ref[...] = jnp.zeros(acc_ref.shape, jnp.float32)

    for s in range(blocks):

        def step(s=s):
            kv = kv_refs[s][...]
            keys = kv[:, :head_dim]
            values = kv[:, head_dim:]
            scores = (
                lax.dot_general(
                    stacked, keys, (((1,), (1,)), ((), ())), preferred_element_type=jnp.float32
                )
                * score_scale
            )
            allowed = segq == segk_ref[s : s + 1, :]
            if s == 0:
                qi = lax.broadcasted_iota(jnp.int32, (rows, rows), 0)
                ki = lax.broadcasted_iota(jnp.int32, (rows, rows), 1)
                allowed = jnp.logical_and(allowed, ki <= qi)
            bias = jnp.where(allowed, 0.0, masked_score).astype(jnp.float32)
            scores = (scores.reshape(group_size, rows, rows) + bias[None]).reshape(
                group_size * rows, rows
            )
            m_old = m_ref[...]
            m_new = jnp.maximum(m_old, jnp.max(scores, axis=1, keepdims=True))
            weights = jnp.exp(scores - m_new)
            factor = jnp.exp(m_old - m_new)
            l_ref[...] = l_ref[...] * factor + jnp.sum(weights, axis=1, keepdims=True)
            acc_ref[...] = acc_ref[...] * factor + jnp.dot(
                weights.astype(jnp.bfloat16), values, preferred_element_type=jnp.float32
            )
            m_ref[...] = m_new

        if s == 0:
            step()
        else:
            pl.when(flags_ref[s] > 0)(step)

    out = acc_ref[...] / l_ref[...]
    for h in range(group_size):
        o_ref[:, h * head_dim : (h + 1) * head_dim] = out[h * rows : (h + 1) * rows].astype(
            o_ref.dtype
        )


def tokens_attention(queries, keys_values, seg_local, helper, help_size):
    local_rows, heads, head_dim = queries.shape
    heads_kv = keys_values.shape[1]
    group_size = heads // heads_kv
    pair = keys_values.shape[2]
    score_scale = 1.0 / math.sqrt(head_dim)
    flat = keys_values.reshape(local_rows, heads_kv * pair)
    seg_row = jnp.zeros((SEG_ROWS, heads_kv * pair), jnp.bfloat16)
    seg_row = seg_row.at[0, :local_rows].set(seg_local.astype(jnp.bfloat16))
    packed = jnp.concatenate([flat, seg_row], axis=0)
    reach = min((MOST - 1 + local_rows - 1) // local_rows, help_size - 1)
    received = [packed]
    for shift in range(1, reach + 1):
        pairs = [(j, j + shift) for j in range(help_size - shift)]
        received.append(lax.ppermute(packed, "help", pairs))
    blocks = len(received)
    segk = jnp.stack(
        [seg_local] + [r[local_rows, :local_rows].astype(jnp.int32) for r in received[1:]]
    )
    first_seg = seg_local[0]
    flags = jnp.stack(
        [jnp.int32(1)]
        + [
            jnp.logical_and(helper >= s, segk[s, local_rows - 1] >= first_seg).astype(jnp.int32)
            for s in range(1, blocks)
        ]
    )
    kernel = functools.partial(
        attention_kernel,
        blocks=blocks,
        group_size=group_size,
        head_dim=head_dim,
        score_scale=score_scale,
    )
    width = group_size * head_dim
    grid_spec = pltpu.PrefetchScalarGridSpec(
        num_scalar_prefetch=1,
        grid=(heads_kv,),
        in_specs=[
            pl.BlockSpec((local_rows, width), lambda g, f: (0, g)),
            pl.BlockSpec((local_rows, 1), lambda g, f: (0, 0)),
            pl.BlockSpec((blocks, local_rows), lambda g, f: (0, 0)),
        ]
        + [pl.BlockSpec((local_rows, pair), lambda g, f: (0, g)) for _ in range(blocks)],
        out_specs=pl.BlockSpec((local_rows, width), lambda g, f: (0, g)),
        scratch_shapes=[
            pltpu.VMEM((group_size * local_rows, 1), jnp.float32),
            pltpu.VMEM((group_size * local_rows, 1), jnp.float32),
            pltpu.VMEM((group_size * local_rows, head_dim), jnp.float32),
        ],
    )
    return pl.pallas_call(
        kernel,
        grid_spec=grid_spec,
        out_shape=jax.ShapeDtypeStruct((local_rows, heads * head_dim), jnp.bfloat16),
        compiler_params=pltpu.CompilerParams(dimension_semantics=("arbitrary",)),
        interpret=INTERPRET,
    )(
        flags,
        queries.reshape(local_rows, heads * head_dim),
        seg_local.reshape(local_rows, 1),
        segk,
        *received,
    )


def make_on_device(help_size):
    partner = [(0, 1), (1, 0)]

    def on_device(queries, keys_values, segment_ids, residual, out_weight):
        local_rows = queries.shape[0]
        width = out_weight.shape[1]
        gathered = lax.all_gather(out_weight, "z", axis=0)
        seg_local = segment_ids.reshape(local_rows)
        helper = lax.axis_index("help")
        core = lax.axis_index("core")
        first = core == 0
        planes = gathered.shape[0]
        stream = residual.reshape(local_rows, planes, 2, width)
        own_cols = jnp.where(first, stream[:, :, 0], stream[:, :, 1])
        other_cols = jnp.where(first, stream[:, :, 1], stream[:, :, 0])
        partner_res = lax.ppermute(other_cols, "core", partner)
        attended = tokens_attention(queries, keys_values, seg_local, helper, help_size)
        partner_att = lax.ppermute(attended, "core", partner)

        def project(rows, res):
            summed = jnp.einsum(
                "qk,zkn->qzn", rows, gathered, preferred_element_type=jnp.float32
            )
            return (res.astype(jnp.float32) + summed).astype(jnp.bfloat16)

        mine = project(attended, own_cols)
        theirs = project(partner_att, partner_res)
        back = lax.ppermute(theirs, "core", partner)
        col0 = jnp.where(first, mine, back)
        col1 = jnp.where(first, back, mine)
        return jnp.stack([col0, col1], axis=2).reshape(local_rows, planes * 2 * width)

    return on_device


def solution(mesh):
    dp_size, help_size = mesh.devices.shape
    split = Mesh(mesh.devices.reshape(dp_size // 2, 2, help_size), ("z", "core", "help"))
    rows = ("z", "core", "help")
    return jax.shard_map(
        make_on_device(help_size),
        mesh=split,
        in_specs=(
            P(rows, None, None),
            P(rows, None, None),
            P(("z", "core"), "help"),
            P(rows, None),
            P(None, ("z", "core")),
        ),
        out_specs=P(rows, None),
        check_vma=False,
    )
```

```python
import functools
import math

import jax
import jax.numpy as jnp
from jax import lax
from jax.experimental import pallas as pl
from jax.experimental.pallas import tpu as pltpu
from jax.sharding import Mesh
from jax.sharding import PartitionSpec as P

masked_score = -1e30
MOST = 2048
SEG_ROWS = 16
INTERPRET = False
QUERY_CHUNK = 128


def attention_kernel(
    flags_ref, q_ref, segq_ref, segk_ref, *refs, blocks, group_size, head_dim, score_scale
):
    kv_refs = refs[:blocks]
    o_ref = refs[blocks]
    m_ref, acc_ref = refs[blocks + 1 :]
    rows = q_ref.shape[0]
    chunks = rows // QUERY_CHUNK
    lanes = m_ref.shape[1]
    exp2_scale = score_scale * math.log2(math.e)
    m_ref[...] = jnp.full(m_ref.shape, masked_score, jnp.float32)
    acc_ref[...] = jnp.zeros(acc_ref.shape, jnp.float32)
    ones = jnp.ones((rows, head_dim), jnp.bfloat16)

    for s in range(blocks):

        def step(s=s):
            keys = kv_refs[s][:, :head_dim]
            values = jnp.concatenate([kv_refs[s][:, head_dim:], ones], axis=1)
            segk = segk_ref[s : s + 1, :]
            for c in range(chunks):
                lo = c * QUERY_CHUNK
                allowed = segq_ref[lo : lo + QUERY_CHUNK, :] == segk
                if s == 0:
                    qi = lax.broadcasted_iota(jnp.int32, (QUERY_CHUNK, rows), 0) + lo
                    ki = lax.broadcasted_iota(jnp.int32, (QUERY_CHUNK, rows), 1)
                    allowed = jnp.logical_and(allowed, ki <= qi)
                bias = jnp.where(allowed, 0.0, masked_score).astype(jnp.float32)
                for h in range(group_size):
                    part = q_ref[lo : lo + QUERY_CHUNK, h * head_dim : (h + 1) * head_dim]
                    scores = (
                        lax.dot_general(
                            part,
                            keys,
                            (((1,), (1,)), ((), ())),
                            preferred_element_type=jnp.float32,
                        )
                        + bias
                    )
                    r = slice(h * rows + lo, h * rows + lo + QUERY_CHUNK)
                    m_old = m_ref[r, :]
                    m_new = jnp.maximum(m_old, jnp.max(scores, axis=1, keepdims=True))
                    wide = jnp.concatenate([m_new] * (rows // lanes), axis=1)
                    weights = jnp.exp2((scores - wide) * exp2_scale)
                    factor = jnp.exp2((m_old - m_new) * exp2_scale)
                    factor = jnp.concatenate([factor] * (2 * head_dim // lanes), axis=1)
                    acc_ref[r, :] = acc_ref[r, :] * factor + jnp.dot(
                        weights.astype(jnp.bfloat16), values, preferred_element_type=jnp.float32
                    )
                    m_ref[r, :] = m_new

        if s == 0:
            step()
        else:
            pl.when(flags_ref[s] > 0)(step)

    for h in range(group_size):
        r = slice(h * rows, (h + 1) * rows)
        acc = acc_ref[r, :]
        o_ref[:, h * head_dim : (h + 1) * head_dim] = (
            acc[:, :head_dim] / acc[:, head_dim:]
        ).astype(o_ref.dtype)


def tokens_attention(queries, keys_values, seg_local, helper, help_size):
    local_rows, heads, head_dim = queries.shape
    heads_kv = keys_values.shape[1]
    group_size = heads // heads_kv
    pair = keys_values.shape[2]
    score_scale = 1.0 / math.sqrt(head_dim)
    flat = keys_values.reshape(local_rows, heads_kv * pair)
    seg_row = jnp.zeros((SEG_ROWS, heads_kv * pair), jnp.bfloat16)
    seg_row = seg_row.at[0, :local_rows].set(seg_local.astype(jnp.bfloat16))
    packed = jnp.concatenate([flat, seg_row], axis=0)
    reach = min((MOST - 1 + local_rows - 1) // local_rows, help_size - 1)
    received = [packed]
    for shift in range(1, reach + 1):
        pairs = [(j, j + shift) for j in range(help_size - shift)]
        received.append(lax.ppermute(packed, "help", pairs))
    blocks = len(received)
    segk = jnp.stack(
        [seg_local] + [r[local_rows, :local_rows].astype(jnp.int32) for r in received[1:]]
    )
    first_seg = seg_local[0]
    flags = jnp.stack(
        [jnp.int32(1)]
        + [
            jnp.logical_and(helper >= s, segk[s, local_rows - 1] >= first_seg).astype(jnp.int32)
            for s in range(1, blocks)
        ]
    )
    kernel = functools.partial(
        attention_kernel,
        blocks=blocks,
        group_size=group_size,
        head_dim=head_dim,
        score_scale=score_scale,
    )
    width = group_size * head_dim
    grid_spec = pltpu.PrefetchScalarGridSpec(
        num_scalar_prefetch=1,
        grid=(heads_kv,),
        in_specs=[
            pl.BlockSpec((local_rows, width), lambda g, f: (0, g)),
            pl.BlockSpec((local_rows, 1), lambda g, f: (0, 0)),
            pl.BlockSpec((blocks, local_rows), lambda g, f: (0, 0)),
        ]
        + [pl.BlockSpec((local_rows, pair), lambda g, f: (0, g)) for _ in range(blocks)],
        out_specs=pl.BlockSpec((local_rows, width), lambda g, f: (0, g)),
        scratch_shapes=[
            pltpu.VMEM((group_size * local_rows, 128), jnp.float32),
            pltpu.VMEM((group_size * local_rows, 2 * head_dim), jnp.float32),
        ],
    )
    return pl.pallas_call(
        kernel,
        grid_spec=grid_spec,
        out_shape=jax.ShapeDtypeStruct((local_rows, heads * head_dim), jnp.bfloat16),
        compiler_params=pltpu.CompilerParams(dimension_semantics=("arbitrary",)),
        interpret=INTERPRET,
    )(
        flags,
        queries.reshape(local_rows, heads * head_dim),
        seg_local.reshape(local_rows, 1),
        segk,
        *received,
    )


def make_on_device(help_size):
    partner = [(0, 1), (1, 0)]

    def on_device(queries, keys_values, segment_ids, residual, out_weight):
        local_rows = queries.shape[0]
        width = out_weight.shape[1]
        gathered = lax.all_gather(out_weight, "z", axis=0)
        seg_local = segment_ids.reshape(local_rows)
        helper = lax.axis_index("help")
        core = lax.axis_index("core")
        first = core == 0
        planes = gathered.shape[0]
        stream = residual.reshape(local_rows, planes, 2, width)
        own_cols = jnp.where(first, stream[:, :, 0], stream[:, :, 1])
        other_cols = jnp.where(first, stream[:, :, 1], stream[:, :, 0])
        partner_res = lax.ppermute(other_cols, "core", partner)
        attended = tokens_attention(queries, keys_values, seg_local, helper, help_size)
        partner_att = lax.ppermute(attended, "core", partner)

        def project(rows, res):
            summed = jnp.einsum(
                "qk,zkn->qzn", rows, gathered, preferred_element_type=jnp.float32
            )
            return (res.astype(jnp.float32) + summed).astype(jnp.bfloat16)

        mine = project(attended, own_cols)
        theirs = project(partner_att, partner_res)
        back = lax.ppermute(theirs, "core", partner)
        col0 = jnp.where(first, mine, back)
        col1 = jnp.where(first, back, mine)
        return jnp.stack([col0, col1], axis=2).reshape(local_rows, planes * 2 * width)

    return on_device


def solution(mesh):
    dp_size, help_size = mesh.devices.shape
    split = Mesh(mesh.devices.reshape(dp_size // 2, 2, help_size), ("z", "core", "help"))
    rows = ("z", "core", "help")
    return jax.shard_map(
        make_on_device(help_size),
        mesh=split,
        in_specs=(
            P(rows, None, None),
            P(rows, None, None),
            P(("z", "core"), "help"),
            P(rows, None),
            P(None, ("z", "core")),
        ),
        out_specs=P(rows, None),
        check_vma=False,
    )
```

```python
import functools
import math

import jax
import jax.numpy as jnp
from jax import lax
from jax.experimental import pallas as pl
from jax.experimental.pallas import tpu as pltpu
from jax.sharding import Mesh
from jax.sharding import PartitionSpec as P

masked_score = -1e30
MOST = 2048
SEG_ROWS = 16
INTERPRET = False
QUERY_CHUNK = 128


def attention_kernel(
    flags_ref, q_ref, segq_ref, segk_ref, *refs, blocks, group_size, head_dim, score_scale
):
    kv_refs = refs[:blocks]
    o_ref = refs[blocks]
    m_ref, acc_ref = refs[blocks + 1 :]
    rows = q_ref.shape[0]
    chunks = rows // QUERY_CHUNK
    lanes = m_ref.shape[1]
    exp2_scale = score_scale * math.log2(math.e)
    m_ref[...] = jnp.full(m_ref.shape, masked_score, jnp.float32)
    acc_ref[...] = jnp.zeros(acc_ref.shape, jnp.float32)
    ones = jnp.ones((rows, head_dim), jnp.bfloat16)

    for s in range(blocks):

        def step(s=s):
            keys = kv_refs[s][:, :head_dim]
            values = jnp.concatenate([kv_refs[s][:, head_dim:], ones], axis=1)
            segk = segk_ref[s : s + 1, :]
            for c in range(chunks):
                lo = c * QUERY_CHUNK
                allowed = segq_ref[lo : lo + QUERY_CHUNK, :] == segk
                if s == 0:
                    qi = lax.broadcasted_iota(jnp.int32, (QUERY_CHUNK, rows), 0) + lo
                    ki = lax.broadcasted_iota(jnp.int32, (QUERY_CHUNK, rows), 1)
                    allowed = jnp.logical_and(allowed, ki <= qi)
                bias = jnp.where(allowed, 0.0, masked_score).astype(jnp.float32)
                for h in range(group_size):
                    part = q_ref[lo : lo + QUERY_CHUNK, h * head_dim : (h + 1) * head_dim]
                    scores = (
                        lax.dot_general(
                            part,
                            keys,
                            (((1,), (1,)), ((), ())),
                            preferred_element_type=jnp.float32,
                        )
                        + bias
                    )
                    r = slice(h * rows + lo, h * rows + lo + QUERY_CHUNK)
                    m_old = m_ref[r, :]
                    m_new = jnp.maximum(m_old, jnp.max(scores, axis=1, keepdims=True))
                    wide = jnp.concatenate([m_new] * (rows // lanes), axis=1)
                    weights = jnp.exp2((scores - wide) * exp2_scale)
                    factor = jnp.exp2((m_old - m_new) * exp2_scale)
                    factor = jnp.concatenate([factor] * (2 * head_dim // lanes), axis=1)
                    acc_ref[r, :] = acc_ref[r, :] * factor + jnp.dot(
                        weights.astype(jnp.bfloat16), values, preferred_element_type=jnp.float32
                    )
                    m_ref[r, :] = m_new

        if s == 0:
            step()
        else:
            pl.when(flags_ref[s] > 0)(step)

    for h in range(group_size):
        r = slice(h * rows, (h + 1) * rows)
        acc = acc_ref[r, :]
        o_ref[:, h * head_dim : (h + 1) * head_dim] = (
            acc[:, :head_dim] / acc[:, head_dim:]
        ).astype(o_ref.dtype)


def tokens_attention(queries, keys_values, seg_local, helper, help_size):
    local_rows, heads, head_dim = queries.shape
    heads_kv = keys_values.shape[1]
    group_size = heads // heads_kv
    pair = keys_values.shape[2]
    score_scale = 1.0 / math.sqrt(head_dim)
    flat = keys_values.reshape(local_rows, heads_kv * pair)
    seg_row = jnp.zeros((SEG_ROWS, heads_kv * pair), jnp.bfloat16)
    seg_row = seg_row.at[0, :local_rows].set(seg_local.astype(jnp.bfloat16))
    packed = jnp.concatenate([flat, seg_row], axis=0)
    reach = min((MOST - 1 + local_rows - 1) // local_rows, help_size - 1)
    across = math.isqrt(help_size)
    one_back = lax.ppermute(
        packed, "help", [(j, j + across) for j in range(help_size - across)]
    )
    two_back = lax.ppermute(
        packed, "help", [(j, j + 2 * across) for j in range(help_size - 2 * across)]
    )
    column = helper % across
    pieces = {0: packed, across: one_back, 2 * across: two_back}
    for k in range(1, across):
        pairs = [
            (y * across + x, y * across + (x + k) % across)
            for y in range(help_size // across)
            for x in range(across)
        ]
        wraps = column + k >= across
        sent = jnp.where(
            wraps, jnp.stack([one_back, two_back]), jnp.stack([packed, one_back])
        )
        got = lax.ppermute(sent, "help", pairs)
        pieces[k] = got[0]
        pieces[k + across] = got[1]
    received = [pieces[s] for s in range(reach + 1)]
    blocks = len(received)
    segk = jnp.stack(
        [seg_local] + [r[local_rows, :local_rows].astype(jnp.int32) for r in received[1:]]
    )
    first_seg = seg_local[0]
    flags = jnp.stack(
        [jnp.int32(1)]
        + [
            jnp.logical_and(helper >= s, segk[s, local_rows - 1] >= first_seg).astype(jnp.int32)
            for s in range(1, blocks)
        ]
    )
    kernel = functools.partial(
        attention_kernel,
        blocks=blocks,
        group_size=group_size,
        head_dim=head_dim,
        score_scale=score_scale,
    )
    width = group_size * head_dim
    grid_spec = pltpu.PrefetchScalarGridSpec(
        num_scalar_prefetch=1,
        grid=(heads_kv,),
        in_specs=[
            pl.BlockSpec((local_rows, width), lambda g, f: (0, g)),
            pl.BlockSpec((local_rows, 1), lambda g, f: (0, 0)),
            pl.BlockSpec((blocks, local_rows), lambda g, f: (0, 0)),
        ]
        + [pl.BlockSpec((local_rows, pair), lambda g, f: (0, g)) for _ in range(blocks)],
        out_specs=pl.BlockSpec((local_rows, width), lambda g, f: (0, g)),
        scratch_shapes=[
            pltpu.VMEM((group_size * local_rows, 128), jnp.float32),
            pltpu.VMEM((group_size * local_rows, 2 * head_dim), jnp.float32),
        ],
    )
    return pl.pallas_call(
        kernel,
        grid_spec=grid_spec,
        out_shape=jax.ShapeDtypeStruct((local_rows, heads * head_dim), jnp.bfloat16),
        compiler_params=pltpu.CompilerParams(dimension_semantics=("arbitrary",)),
        interpret=INTERPRET,
    )(
        flags,
        queries.reshape(local_rows, heads * head_dim),
        seg_local.reshape(local_rows, 1),
        segk,
        *received,
    )


def make_on_device(help_size):
    partner = [(0, 1), (1, 0)]

    def on_device(queries, keys_values, segment_ids, residual, out_weight):
        local_rows = queries.shape[0]
        width = out_weight.shape[1]
        gathered = lax.all_gather(out_weight, "z", axis=0)
        seg_local = segment_ids.reshape(local_rows)
        helper = lax.axis_index("help")
        core = lax.axis_index("core")
        first = core == 0
        planes = gathered.shape[0]
        stream = residual.reshape(local_rows, planes, 2, width)
        own_cols = jnp.where(first, stream[:, :, 0], stream[:, :, 1])
        other_cols = jnp.where(first, stream[:, :, 1], stream[:, :, 0])
        partner_res = lax.ppermute(other_cols, "core", partner)
        attended = tokens_attention(queries, keys_values, seg_local, helper, help_size)
        partner_att = lax.ppermute(attended, "core", partner)

        def project(rows, res):
            summed = jnp.einsum(
                "qk,zkn->qzn", rows, gathered, preferred_element_type=jnp.float32
            )
            return (res.astype(jnp.float32) + summed).astype(jnp.bfloat16)

        mine = project(attended, own_cols)
        theirs = project(partner_att, partner_res)
        back = lax.ppermute(theirs, "core", partner)
        col0 = jnp.where(first, mine, back)
        col1 = jnp.where(first, back, mine)
        return jnp.stack([col0, col1], axis=2).reshape(local_rows, planes * 2 * width)

    return on_device


def solution(mesh):
    dp_size, help_size = mesh.devices.shape
    split = Mesh(mesh.devices.reshape(dp_size // 2, 2, help_size), ("z", "core", "help"))
    rows = ("z", "core", "help")
    return jax.shard_map(
        make_on_device(help_size),
        mesh=split,
        in_specs=(
            P(rows, None, None),
            P(rows, None, None),
            P(("z", "core"), "help"),
            P(rows, None),
            P(None, ("z", "core")),
        ),
        out_specs=P(rows, None),
        check_vma=False,
    )
```

```python
import functools
import math

import jax
import jax.numpy as jnp
from jax import lax
from jax.experimental import pallas as pl
from jax.experimental.pallas import tpu as pltpu
from jax.sharding import Mesh
from jax.sharding import PartitionSpec as P

masked_score = -1e30
MOST = 2048
SEG_ROWS = 16
INTERPRET = False
QUERY_CHUNK = 128


def attention_kernel(
    flags_ref, q_ref, segq_ref, segk_ref, *refs, blocks, group_size, head_dim, score_scale
):
    kv_refs = refs[:blocks]
    o_ref = refs[blocks]
    m_ref, acc_ref = refs[blocks + 1 :]
    rows = q_ref.shape[0]
    chunks = rows // QUERY_CHUNK
    lanes = m_ref.shape[1]
    exp2_scale = score_scale * math.log2(math.e)
    m_ref[...] = jnp.full(m_ref.shape, masked_score, jnp.float32)
    acc_ref[...] = jnp.zeros(acc_ref.shape, jnp.float32)
    ones = jnp.ones((rows, head_dim), jnp.bfloat16)

    for s in range(blocks):

        def step(s=s):
            keys = kv_refs[s][:, :head_dim]
            values = jnp.concatenate([kv_refs[s][:, head_dim:], ones], axis=1)
            segk = segk_ref[s : s + 1, :]
            for c in range(chunks):
                lo = c * QUERY_CHUNK
                allowed = segq_ref[lo : lo + QUERY_CHUNK, :] == segk
                if s == 0:
                    qi = lax.broadcasted_iota(jnp.int32, (QUERY_CHUNK, rows), 0) + lo
                    ki = lax.broadcasted_iota(jnp.int32, (QUERY_CHUNK, rows), 1)
                    allowed = jnp.logical_and(allowed, ki <= qi)
                bias = jnp.where(allowed, 0.0, masked_score).astype(jnp.float32)
                for h in range(group_size):
                    part = q_ref[lo : lo + QUERY_CHUNK, h * head_dim : (h + 1) * head_dim]
                    scores = (
                        lax.dot_general(
                            part,
                            keys,
                            (((1,), (1,)), ((), ())),
                            preferred_element_type=jnp.float32,
                        )
                        + bias
                    )
                    r = slice(h * rows + lo, h * rows + lo + QUERY_CHUNK)
                    m_old = m_ref[r, :]
                    m_new = jnp.maximum(m_old, jnp.max(scores, axis=1, keepdims=True))
                    wide = jnp.concatenate([m_new] * (rows // lanes), axis=1)
                    weights = jnp.exp2((scores - wide) * exp2_scale)
                    factor = jnp.exp2((m_old - m_new) * exp2_scale)
                    factor = jnp.concatenate([factor] * (2 * head_dim // lanes), axis=1)
                    acc_ref[r, :] = acc_ref[r, :] * factor + jnp.dot(
                        weights.astype(jnp.bfloat16), values, preferred_element_type=jnp.float32
                    )
                    m_ref[r, :] = m_new

        if s == 0:
            step()
        else:
            pl.when(flags_ref[s] > 0)(step)

    for h in range(group_size):
        r = slice(h * rows, (h + 1) * rows)
        acc = acc_ref[r, :]
        o_ref[:, h * head_dim : (h + 1) * head_dim] = (
            acc[:, :head_dim] / acc[:, head_dim:]
        ).astype(o_ref.dtype)


def tokens_attention(queries, keys_values, seg_local, helper, help_size):
    local_rows, heads, head_dim = queries.shape
    heads_kv = keys_values.shape[1]
    group_size = heads // heads_kv
    pair = keys_values.shape[2]
    score_scale = 1.0 / math.sqrt(head_dim)
    flat = keys_values.reshape(local_rows, heads_kv * pair)
    seg_row = jnp.zeros((SEG_ROWS, heads_kv * pair), jnp.bfloat16)
    seg_row = seg_row.at[0, :local_rows].set(seg_local.astype(jnp.bfloat16))
    packed = jnp.concatenate([flat, seg_row], axis=0)
    reach = min((MOST - 1 + local_rows - 1) // local_rows, help_size - 1)
    across = math.isqrt(help_size)
    one_back = lax.ppermute(
        packed, "help", [(j, j + across) for j in range(help_size - across)]
    )
    two_back = lax.ppermute(
        packed, "help", [(j, j + 2 * across) for j in range(help_size - 2 * across)]
    )
    column = helper % across
    pieces = {0: (packed, None), across: (one_back, None), 2 * across: (two_back, None)}
    for k in range(1, across):
        pairs = [
            (y * across + x, y * across + (x + k) % across)
            for y in range(help_size // across)
            for x in range(across)
        ]
        wraps = column + k >= across
        sent = jnp.where(
            wraps, jnp.stack([one_back, two_back]), jnp.stack([packed, one_back])
        )
        got = lax.ppermute(sent, "help", pairs)
        pieces[k] = (got, 0)
        pieces[k + across] = (got, 1)
    received = [pieces[s] for s in range(reach + 1)]
    blocks = len(received)

    def seg_of(piece):
        array, index = piece
        row = array[local_rows] if index is None else array[index, local_rows]
        return row[:local_rows].astype(jnp.int32)

    segk = jnp.stack([seg_local] + [seg_of(p) for p in received[1:]])
    first_seg = seg_local[0]
    flags = jnp.stack(
        [jnp.int32(1)]
        + [
            jnp.logical_and(helper >= s, segk[s, local_rows - 1] >= first_seg).astype(jnp.int32)
            for s in range(1, blocks)
        ]
    )
    kernel = functools.partial(
        attention_kernel,
        blocks=blocks,
        group_size=group_size,
        head_dim=head_dim,
        score_scale=score_scale,
    )
    width = group_size * head_dim
    grid_spec = pltpu.PrefetchScalarGridSpec(
        num_scalar_prefetch=1,
        grid=(heads_kv,),
        in_specs=[
            pl.BlockSpec((local_rows, width), lambda g, f: (0, g)),
            pl.BlockSpec((local_rows, 1), lambda g, f: (0, 0)),
            pl.BlockSpec((blocks, local_rows), lambda g, f: (0, 0)),
        ]
        + [
            pl.BlockSpec((local_rows, pair), lambda g, f: (0, g))
            if index is None
            else pl.BlockSpec((None, local_rows, pair), lambda g, f, i=index: (i, 0, g))
            for _, index in received
        ],
        out_specs=pl.BlockSpec((local_rows, width), lambda g, f: (0, g)),
        scratch_shapes=[
            pltpu.VMEM((group_size * local_rows, 128), jnp.float32),
            pltpu.VMEM((group_size * local_rows, 2 * head_dim), jnp.float32),
        ],
    )
    return pl.pallas_call(
        kernel,
        grid_spec=grid_spec,
        out_shape=jax.ShapeDtypeStruct((local_rows, heads * head_dim), jnp.bfloat16),
        compiler_params=pltpu.CompilerParams(dimension_semantics=("arbitrary",)),
        interpret=INTERPRET,
    )(
        flags,
        queries.reshape(local_rows, heads * head_dim),
        seg_local.reshape(local_rows, 1),
        segk,
        *[array for array, _ in received],
    )


def make_on_device(help_size):
    partner = [(0, 1), (1, 0)]

    def on_device(queries, keys_values, segment_ids, residual, out_weight):
        local_rows = queries.shape[0]
        width = out_weight.shape[1]
        gathered = lax.all_gather(out_weight, "z", axis=0)
        seg_local = segment_ids.reshape(local_rows)
        helper = lax.axis_index("help")
        core = lax.axis_index("core")
        first = core == 0
        planes = gathered.shape[0]
        stream = residual.reshape(local_rows, planes, 2, width)
        own_cols = jnp.where(first, stream[:, :, 0], stream[:, :, 1])
        other_cols = jnp.where(first, stream[:, :, 1], stream[:, :, 0])
        partner_res = lax.ppermute(other_cols, "core", partner)
        attended = tokens_attention(queries, keys_values, seg_local, helper, help_size)
        partner_att = lax.ppermute(attended, "core", partner)

        def project(rows, res):
            summed = jnp.einsum(
                "qk,zkn->qzn", rows, gathered, preferred_element_type=jnp.float32
            )
            return (res.astype(jnp.float32) + summed).astype(jnp.bfloat16)

        mine = project(attended, own_cols)
        theirs = project(partner_att, partner_res)
        back = lax.ppermute(theirs, "core", partner)
        joined = lax.cond(
            first,
            lambda: jnp.stack([mine, back], axis=2),
            lambda: jnp.stack([back, mine], axis=2),
        )
        return joined.reshape(local_rows, planes * 2 * width)

    return on_device


def solution(mesh):
    dp_size, help_size = mesh.devices.shape
    split = Mesh(mesh.devices.reshape(dp_size // 2, 2, help_size), ("z", "core", "help"))
    rows = ("z", "core", "help")
    return jax.shard_map(
        make_on_device(help_size),
        mesh=split,
        in_specs=(
            P(rows, None, None),
            P(rows, None, None),
            P(("z", "core"), "help"),
            P(rows, None),
            P(None, ("z", "core")),
        ),
        out_specs=P(rows, None),
        check_vma=False,
    )
```

```python
import functools
import math

import jax
import jax.numpy as jnp
from jax import lax
from jax.experimental import pallas as pl
from jax.experimental.pallas import tpu as pltpu
from jax.sharding import Mesh
from jax.sharding import PartitionSpec as P

masked_score = -1e30
MOST = 2048
SEG_ROWS = 16
INTERPRET = False
QUERY_CHUNK = 128


def attention_kernel(
    flags_ref, q_ref, segq_ref, segk_ref, *refs, blocks, group_size, head_dim, score_scale
):
    kv_refs = refs[:blocks]
    o_ref = refs[blocks]
    m_ref, acc_ref = refs[blocks + 1 :]
    rows = q_ref.shape[0]
    chunks = rows // QUERY_CHUNK
    lanes = m_ref.shape[1]
    exp2_scale = score_scale * math.log2(math.e)
    m_ref[...] = jnp.full(m_ref.shape, masked_score, jnp.float32)
    acc_ref[...] = jnp.zeros(acc_ref.shape, jnp.float32)
    ones = jnp.ones((rows, head_dim), jnp.bfloat16)

    for s in range(blocks):

        def step(s=s):
            keys = kv_refs[s][:, :head_dim]
            values = jnp.concatenate([kv_refs[s][:, head_dim:], ones], axis=1)
            segk = segk_ref[s : s + 1, :]
            for c in range(chunks):
                lo = c * QUERY_CHUNK
                allowed = segq_ref[lo : lo + QUERY_CHUNK, :] == segk
                if s == 0:
                    qi = lax.broadcasted_iota(jnp.int32, (QUERY_CHUNK, rows), 0) + lo
                    ki = lax.broadcasted_iota(jnp.int32, (QUERY_CHUNK, rows), 1)
                    allowed = jnp.logical_and(allowed, ki <= qi)
                bias = jnp.where(allowed, 0.0, masked_score).astype(jnp.float32)
                for h in range(group_size):
                    part = q_ref[lo : lo + QUERY_CHUNK, h * head_dim : (h + 1) * head_dim]
                    scores = (
                        lax.dot_general(
                            part,
                            keys,
                            (((1,), (1,)), ((), ())),
                            preferred_element_type=jnp.float32,
                        )
                        + bias
                    )
                    r = slice(h * rows + lo, h * rows + lo + QUERY_CHUNK)
                    m_old = m_ref[r, :]
                    m_new = jnp.maximum(m_old, jnp.max(scores, axis=1, keepdims=True))
                    wide = jnp.concatenate([m_new] * (rows // lanes), axis=1)
                    weights = jnp.exp2((scores - wide) * exp2_scale)
                    factor = jnp.exp2((m_old - m_new) * exp2_scale)
                    factor = jnp.concatenate([factor] * (2 * head_dim // lanes), axis=1)
                    acc_ref[r, :] = acc_ref[r, :] * factor + jnp.dot(
                        weights.astype(jnp.bfloat16), values, preferred_element_type=jnp.float32
                    )
                    m_ref[r, :] = m_new

        if s == 0:
            step()
        else:
            pl.when(flags_ref[s] > 0)(step)

    for h in range(group_size):
        r = slice(h * rows, (h + 1) * rows)
        acc = acc_ref[r, :]
        o_ref[:, h * head_dim : (h + 1) * head_dim] = (
            acc[:, :head_dim] / acc[:, head_dim:]
        ).astype(o_ref.dtype)


def tokens_attention(queries, keys_values, seg_local, helper, help_size):
    local_rows, heads, head_dim = queries.shape
    heads_kv = keys_values.shape[1]
    group_size = heads // heads_kv
    pair = keys_values.shape[2]
    score_scale = 1.0 / math.sqrt(head_dim)
    flat = keys_values.reshape(local_rows, heads_kv * pair)
    seg_row = jnp.zeros((SEG_ROWS, heads_kv * pair), jnp.bfloat16)
    seg_row = seg_row.at[0, :local_rows].set(seg_local.astype(jnp.bfloat16))
    packed = jnp.concatenate([flat, seg_row], axis=0)
    reach = min((MOST - 1 + local_rows - 1) // local_rows, help_size - 1)
    across = math.isqrt(help_size)
    one_back = lax.ppermute(
        packed, "help", [(j, j + across) for j in range(help_size - across)]
    )
    two_back = lax.ppermute(
        packed, "help", [(j, j + 2 * across) for j in range(help_size - 2 * across)]
    )
    column = helper % across
    rows_of = help_size // across
    pieces = {0: (packed, None), across: (one_back, None), 2 * across: (two_back, None)}
    for k in range(1, across):
        ring = lambda xs: [
            (y * across + x, y * across + (x + k) % across) for y in range(rows_of) for x in xs
        ]
        early = lax.ppermute(packed, "help", ring(range(across - k)))
        late_one = lax.ppermute(one_back, "help", ring(range(across)))
        late_two = lax.ppermute(two_back, "help", ring(range(across - k, across)))
        direct = column >= k
        pieces[k] = (jnp.where(direct, early, late_one), None)
        pieces[k + across] = (jnp.where(direct, late_one, late_two), None)
    received = [pieces[s] for s in range(reach + 1)]
    blocks = len(received)

    def seg_of(piece):
        array, index = piece
        row = array[local_rows] if index is None else array[index, local_rows]
        return row[:local_rows].astype(jnp.int32)

    segk = jnp.stack([seg_local] + [seg_of(p) for p in received[1:]])
    first_seg = seg_local[0]
    flags = jnp.stack(
        [jnp.int32(1)]
        + [
            jnp.logical_and(helper >= s, segk[s, local_rows - 1] >= first_seg).astype(jnp.int32)
            for s in range(1, blocks)
        ]
    )
    kernel = functools.partial(
        attention_kernel,
        blocks=blocks,
        group_size=group_size,
        head_dim=head_dim,
        score_scale=score_scale,
    )
    width = group_size * head_dim
    grid_spec = pltpu.PrefetchScalarGridSpec(
        num_scalar_prefetch=1,
        grid=(heads_kv,),
        in_specs=[
            pl.BlockSpec((local_rows, width), lambda g, f: (0, g)),
            pl.BlockSpec((local_rows, 1), lambda g, f: (0, 0)),
            pl.BlockSpec((blocks, local_rows), lambda g, f: (0, 0)),
        ]
        + [
            pl.BlockSpec((local_rows, pair), lambda g, f: (0, g))
            if index is None
            else pl.BlockSpec((None, local_rows, pair), lambda g, f, i=index: (i, 0, g))
            for _, index in received
        ],
        out_specs=pl.BlockSpec((local_rows, width), lambda g, f: (0, g)),
        scratch_shapes=[
            pltpu.VMEM((group_size * local_rows, 128), jnp.float32),
            pltpu.VMEM((group_size * local_rows, 2 * head_dim), jnp.float32),
        ],
    )
    return pl.pallas_call(
        kernel,
        grid_spec=grid_spec,
        out_shape=jax.ShapeDtypeStruct((local_rows, heads * head_dim), jnp.bfloat16),
        compiler_params=pltpu.CompilerParams(dimension_semantics=("arbitrary",)),
        interpret=INTERPRET,
    )(
        flags,
        queries.reshape(local_rows, heads * head_dim),
        seg_local.reshape(local_rows, 1),
        segk,
        *[array for array, _ in received],
    )


def make_on_device(help_size):
    partner = [(0, 1), (1, 0)]

    def on_device(queries, keys_values, segment_ids, residual, out_weight):
        local_rows = queries.shape[0]
        width = out_weight.shape[1]
        gathered = lax.all_gather(out_weight, "z", axis=0)
        seg_local = segment_ids.reshape(local_rows)
        helper = lax.axis_index("help")
        core = lax.axis_index("core")
        first = core == 0
        planes = gathered.shape[0]
        stream = residual.reshape(local_rows, planes, 2, width)
        own_cols = jnp.where(first, stream[:, :, 0], stream[:, :, 1])
        other_cols = jnp.where(first, stream[:, :, 1], stream[:, :, 0])
        partner_res = lax.ppermute(other_cols, "core", partner)
        attended = tokens_attention(queries, keys_values, seg_local, helper, help_size)
        partner_att = lax.ppermute(attended, "core", partner)

        def project(rows, res):
            summed = jnp.einsum(
                "qk,zkn->qzn", rows, gathered, preferred_element_type=jnp.float32
            )
            return (res.astype(jnp.float32) + summed).astype(jnp.bfloat16)

        mine = project(attended, own_cols)
        theirs = project(partner_att, partner_res)
        back = lax.ppermute(theirs, "core", partner)
        col0 = jnp.where(first, mine, back)
        col1 = jnp.where(first, back, mine)
        return jnp.stack([col0, col1], axis=2).reshape(local_rows, planes * 2 * width)

    return on_device


def solution(mesh):
    dp_size, help_size = mesh.devices.shape
    split = Mesh(mesh.devices.reshape(dp_size // 2, 2, help_size), ("z", "core", "help"))
    rows = ("z", "core", "help")
    return jax.shard_map(
        make_on_device(help_size),
        mesh=split,
        in_specs=(
            P(rows, None, None),
            P(rows, None, None),
            P(("z", "core"), "help"),
            P(rows, None),
            P(None, ("z", "core")),
        ),
        out_specs=P(rows, None),
        check_vma=False,
    )
```

```python
import functools
import math

import jax
import jax.numpy as jnp
from jax import lax
from jax.experimental import pallas as pl
from jax.experimental.pallas import tpu as pltpu
from jax.sharding import Mesh
from jax.sharding import PartitionSpec as P

masked_score = -1e30
MOST = 2048
SEG_ROWS = 16
INTERPRET = False
QUERY_CHUNK = 128


def attention_kernel(
    flags_ref, q_ref, segq_ref, segk_ref, *refs, layout, group_size, head_dim, score_scale
):
    blocks = len(layout)
    count = sum(layout)
    kv_refs = []
    for s, n in enumerate(layout):
        kv_refs.append(refs[sum(layout[:s]) : sum(layout[:s]) + n])
    o_ref = refs[count]
    m_ref, acc_ref = refs[count + 1 :]
    rows = q_ref.shape[0]
    chunks = rows // QUERY_CHUNK
    lanes = m_ref.shape[1]
    exp2_scale = score_scale * math.log2(math.e)
    m_ref[...] = jnp.full(m_ref.shape, masked_score, jnp.float32)
    acc_ref[...] = jnp.zeros(acc_ref.shape, jnp.float32)
    ones = jnp.ones((rows, head_dim), jnp.bfloat16)

    for s in range(blocks):

        def step(s=s):
            if len(kv_refs[s]) == 1:
                kv = kv_refs[s][0][...]
            else:
                pick = jnp.full(kv_refs[s][0].shape, flags_ref[blocks + s], jnp.int32)
                kv = jnp.where(pick > 0, kv_refs[s][0][...], kv_refs[s][1][...])
            keys = kv[:, :head_dim]
            values = jnp.concatenate([kv[:, head_dim:], ones], axis=1)
            segk = segk_ref[s : s + 1, :]
            for c in range(chunks):
                lo = c * QUERY_CHUNK
                allowed = segq_ref[lo : lo + QUERY_CHUNK, :] == segk
                if s == 0:
                    qi = lax.broadcasted_iota(jnp.int32, (QUERY_CHUNK, rows), 0) + lo
                    ki = lax.broadcasted_iota(jnp.int32, (QUERY_CHUNK, rows), 1)
                    allowed = jnp.logical_and(allowed, ki <= qi)
                bias = jnp.where(allowed, 0.0, masked_score).astype(jnp.float32)
                for h in range(group_size):
                    part = q_ref[lo : lo + QUERY_CHUNK, h * head_dim : (h + 1) * head_dim]
                    scores = (
                        lax.dot_general(
                            part,
                            keys,
                            (((1,), (1,)), ((), ())),
                            preferred_element_type=jnp.float32,
                        )
                        + bias
                    )
                    r = slice(h * rows + lo, h * rows + lo + QUERY_CHUNK)
                    m_old = m_ref[r, :]
                    m_new = jnp.maximum(m_old, jnp.max(scores, axis=1, keepdims=True))
                    wide = jnp.concatenate([m_new] * (rows // lanes), axis=1)
                    weights = jnp.exp2((scores - wide) * exp2_scale)
                    factor = jnp.exp2((m_old - m_new) * exp2_scale)
                    factor = jnp.concatenate([factor] * (2 * head_dim // lanes), axis=1)
                    acc_ref[r, :] = acc_ref[r, :] * factor + jnp.dot(
                        weights.astype(jnp.bfloat16), values, preferred_element_type=jnp.float32
                    )
                    m_ref[r, :] = m_new

        if s == 0:
            step()
        else:
            pl.when(flags_ref[s] > 0)(step)

    for h in range(group_size):
        r = slice(h * rows, (h + 1) * rows)
        acc = acc_ref[r, :]
        o_ref[:, h * head_dim : (h + 1) * head_dim] = (
            acc[:, :head_dim] / acc[:, head_dim:]
        ).astype(o_ref.dtype)


def tokens_attention(queries, keys_values, seg_local, helper, help_size):
    local_rows, heads, head_dim = queries.shape
    heads_kv = keys_values.shape[1]
    group_size = heads // heads_kv
    pair = keys_values.shape[2]
    score_scale = 1.0 / math.sqrt(head_dim)
    flat = keys_values.reshape(local_rows, heads_kv * pair)
    seg_row = jnp.zeros((SEG_ROWS, heads_kv * pair), jnp.bfloat16)
    seg_row = seg_row.at[0, :local_rows].set(seg_local.astype(jnp.bfloat16))
    packed = jnp.concatenate([flat, seg_row], axis=0)
    reach = min((MOST - 1 + local_rows - 1) // local_rows, help_size - 1)
    across = math.isqrt(help_size)
    one_back = lax.ppermute(
        packed, "help", [(j, j + across) for j in range(help_size - across)]
    )
    two_back = lax.ppermute(
        packed, "help", [(j, j + 2 * across) for j in range(help_size - 2 * across)]
    )
    column = helper % across
    rows_of = help_size // across
    pieces = {0: ((packed,), True), across: ((one_back,), True), 2 * across: ((two_back,), True)}
    for k in range(1, across):
        ring = lambda xs: [
            (y * across + x, y * across + (x + k) % across) for y in range(rows_of) for x in xs
        ]
        early = lax.ppermute(packed, "help", ring(range(across - k)))
        late_one = lax.ppermute(one_back, "help", ring(range(across)))
        late_two = lax.ppermute(two_back, "help", ring(range(across - k, across)))
        direct = column >= k
        pieces[k] = ((early, late_one), direct)
        pieces[k + across] = ((late_one, late_two), direct)
    received = [pieces[s] for s in range(reach + 1)]
    blocks = len(received)

    def seg_of(piece):
        arrays, direct = piece
        rows = [a[local_rows, :local_rows].astype(jnp.int32) for a in arrays]
        return rows[0] if len(rows) == 1 else jnp.where(direct, rows[0], rows[1])

    segk = jnp.stack([seg_local] + [seg_of(p) for p in received[1:]])
    picks = [jnp.asarray(direct, jnp.int32) for _, direct in received]
    first_seg = seg_local[0]
    flags = jnp.stack(
        [jnp.int32(1)]
        + [
            jnp.logical_and(helper >= s, segk[s, local_rows - 1] >= first_seg).astype(jnp.int32)
            for s in range(1, blocks)
        ]
        + picks
    )
    kernel = functools.partial(
        attention_kernel,
        layout=tuple(len(arrays) for arrays, _ in received),
        group_size=group_size,
        head_dim=head_dim,
        score_scale=score_scale,
    )
    width = group_size * head_dim
    grid_spec = pltpu.PrefetchScalarGridSpec(
        num_scalar_prefetch=1,
        grid=(heads_kv,),
        in_specs=[
            pl.BlockSpec((local_rows, width), lambda g, f: (0, g)),
            pl.BlockSpec((local_rows, 1), lambda g, f: (0, 0)),
            pl.BlockSpec((blocks, local_rows), lambda g, f: (0, 0)),
        ]
        + [
            pl.BlockSpec((local_rows, pair), lambda g, f: (0, g))
            for arrays, _ in received
            for _ in arrays
        ],
        out_specs=pl.BlockSpec((local_rows, width), lambda g, f: (0, g)),
        scratch_shapes=[
            pltpu.VMEM((group_size * local_rows, 128), jnp.float32),
            pltpu.VMEM((group_size * local_rows, 2 * head_dim), jnp.float32),
        ],
    )
    return pl.pallas_call(
        kernel,
        grid_spec=grid_spec,
        out_shape=jax.ShapeDtypeStruct((local_rows, heads * head_dim), jnp.bfloat16),
        compiler_params=pltpu.CompilerParams(dimension_semantics=("arbitrary",)),
        interpret=INTERPRET,
    )(
        flags,
        queries.reshape(local_rows, heads * head_dim),
        seg_local.reshape(local_rows, 1),
        segk,
        *[array for arrays, _ in received for array in arrays],
    )


def make_on_device(help_size):
    partner = [(0, 1), (1, 0)]

    def on_device(queries, keys_values, segment_ids, residual, out_weight):
        local_rows = queries.shape[0]
        width = out_weight.shape[1]
        gathered = lax.all_gather(out_weight, "z", axis=0)
        seg_local = segment_ids.reshape(local_rows)
        helper = lax.axis_index("help")
        core = lax.axis_index("core")
        first = core == 0
        planes = gathered.shape[0]
        stream = residual.reshape(local_rows, planes, 2, width)
        own_cols = jnp.where(first, stream[:, :, 0], stream[:, :, 1])
        other_cols = jnp.where(first, stream[:, :, 1], stream[:, :, 0])
        partner_res = lax.ppermute(other_cols, "core", partner)
        attended = tokens_attention(queries, keys_values, seg_local, helper, help_size)
        partner_att = lax.ppermute(attended, "core", partner)

        def project(rows, res):
            summed = jnp.einsum(
                "qk,zkn->qzn", rows, gathered, preferred_element_type=jnp.float32
            )
            return (res.astype(jnp.float32) + summed).astype(jnp.bfloat16)

        mine = project(attended, own_cols)
        theirs = project(partner_att, partner_res)
        back = lax.ppermute(theirs, "core", partner)
        col0 = jnp.where(first, mine, back)
        col1 = jnp.where(first, back, mine)
        return jnp.stack([col0, col1], axis=2).reshape(local_rows, planes * 2 * width)

    return on_device


def solution(mesh):
    dp_size, help_size = mesh.devices.shape
    split = Mesh(mesh.devices.reshape(dp_size // 2, 2, help_size), ("z", "core", "help"))
    rows = ("z", "core", "help")
    return jax.shard_map(
        make_on_device(help_size),
        mesh=split,
        in_specs=(
            P(rows, None, None),
            P(rows, None, None),
            P(("z", "core"), "help"),
            P(rows, None),
            P(None, ("z", "core")),
        ),
        out_specs=P(rows, None),
        check_vma=False,
    )
```

```python
import functools
import math

import jax
import jax.numpy as jnp
from jax import lax
from jax.experimental import pallas as pl
from jax.experimental.pallas import tpu as pltpu
from jax.sharding import Mesh
from jax.sharding import PartitionSpec as P

masked_score = -1e30
MOST = 2048
SEG_ROWS = 16
INTERPRET = False
QUERY_CHUNK = 128


def attention_kernel(
    flags_ref, q_ref, segq_ref, segk_ref, *refs, layout, group_size, head_dim, score_scale
):
    blocks = len(layout)
    count = sum(layout)
    kv_refs = []
    for s, n in enumerate(layout):
        kv_refs.append(refs[sum(layout[:s]) : sum(layout[:s]) + n])
    o_ref = refs[count]
    m_ref, acc_ref = refs[count + 1 :]
    rows = q_ref.shape[0]
    chunks = rows // QUERY_CHUNK
    lanes = m_ref.shape[1]
    exp2_scale = score_scale * math.log2(math.e)
    m_ref[...] = jnp.full(m_ref.shape, masked_score, jnp.float32)
    acc_ref[...] = jnp.zeros(acc_ref.shape, jnp.float32)
    ones = jnp.ones((rows, head_dim), jnp.bfloat16)
    head = pl.program_id(0)

    for s in range(blocks):

        def step(s=s):
            if len(kv_refs[s]) == 1:
                kv = kv_refs[s][0][head, :rows, :]
            else:
                first = kv_refs[s][0][head, :rows, :]
                pick = jnp.full(first.shape, flags_ref[blocks + s], jnp.int32)
                kv = jnp.where(pick > 0, first, kv_refs[s][1][head, :rows, :])
            keys = kv[:, :head_dim]
            values = jnp.concatenate([kv[:, head_dim:], ones], axis=1)
            segk = segk_ref[s : s + 1, :]
            for c in range(chunks):
                lo = c * QUERY_CHUNK
                allowed = segq_ref[lo : lo + QUERY_CHUNK, :] == segk
                if s == 0:
                    qi = lax.broadcasted_iota(jnp.int32, (QUERY_CHUNK, rows), 0) + lo
                    ki = lax.broadcasted_iota(jnp.int32, (QUERY_CHUNK, rows), 1)
                    allowed = jnp.logical_and(allowed, ki <= qi)
                bias = jnp.where(allowed, 0.0, masked_score).astype(jnp.float32)
                for h in range(group_size):
                    part = q_ref[lo : lo + QUERY_CHUNK, h * head_dim : (h + 1) * head_dim]
                    scores = (
                        lax.dot_general(
                            part,
                            keys,
                            (((1,), (1,)), ((), ())),
                            preferred_element_type=jnp.float32,
                        )
                        + bias
                    )
                    r = slice(h * rows + lo, h * rows + lo + QUERY_CHUNK)
                    m_old = m_ref[r, :]
                    m_new = jnp.maximum(m_old, jnp.max(scores, axis=1, keepdims=True))
                    wide = jnp.concatenate([m_new] * (rows // lanes), axis=1)
                    weights = jnp.exp2((scores - wide) * exp2_scale)
                    factor = jnp.exp2((m_old - m_new) * exp2_scale)
                    factor = jnp.concatenate([factor] * (2 * head_dim // lanes), axis=1)
                    acc_ref[r, :] = acc_ref[r, :] * factor + jnp.dot(
                        weights.astype(jnp.bfloat16), values, preferred_element_type=jnp.float32
                    )
                    m_ref[r, :] = m_new

        if s == 0:
            step()
        else:
            pl.when(flags_ref[s] > 0)(step)

    for h in range(group_size):
        r = slice(h * rows, (h + 1) * rows)
        acc = acc_ref[r, :]
        o_ref[:, h * head_dim : (h + 1) * head_dim] = (
            acc[:, :head_dim] / acc[:, head_dim:]
        ).astype(o_ref.dtype)


def tokens_attention(queries, keys_values, seg_local, helper, help_size):
    local_rows, heads, head_dim = queries.shape
    heads_kv = keys_values.shape[1]
    group_size = heads // heads_kv
    pair = keys_values.shape[2]
    score_scale = 1.0 / math.sqrt(head_dim)
    flat = jnp.transpose(keys_values, (1, 0, 2))
    seg_row = jnp.zeros((heads_kv, SEG_ROWS, pair), jnp.bfloat16)
    seg_row = seg_row.at[0, 0, :local_rows].set(seg_local.astype(jnp.bfloat16))
    packed = jnp.concatenate([flat, seg_row], axis=1)
    reach = min((MOST - 1 + local_rows - 1) // local_rows, help_size - 1)
    across = math.isqrt(help_size)
    one_back = lax.ppermute(
        packed, "help", [(j, j + across) for j in range(help_size - across)]
    )
    two_back = lax.ppermute(
        packed, "help", [(j, j + 2 * across) for j in range(help_size - 2 * across)]
    )
    column = helper % across
    rows_of = help_size // across
    pieces = {0: ((packed,), True), across: ((one_back,), True), 2 * across: ((two_back,), True)}
    for k in range(1, across):
        ring = lambda xs: [
            (y * across + x, y * across + (x + k) % across) for y in range(rows_of) for x in xs
        ]
        early = lax.ppermute(packed, "help", ring(range(across - k)))
        late_one = lax.ppermute(one_back, "help", ring(range(across)))
        late_two = lax.ppermute(two_back, "help", ring(range(across - k, across)))
        direct = column >= k
        pieces[k] = ((early, late_one), direct)
        pieces[k + across] = ((late_one, late_two), direct)
    received = [pieces[s] for s in range(reach + 1)]
    blocks = len(received)

    def seg_of(piece):
        arrays, direct = piece
        rows = [a[0, local_rows, :local_rows].astype(jnp.int32) for a in arrays]
        return rows[0] if len(rows) == 1 else jnp.where(direct, rows[0], rows[1])

    segk = jnp.stack([seg_local] + [seg_of(p) for p in received[1:]])
    picks = [jnp.asarray(direct, jnp.int32) for _, direct in received]
    first_seg = seg_local[0]
    flags = jnp.stack(
        [jnp.int32(1)]
        + [
            jnp.logical_and(helper >= s, segk[s, local_rows - 1] >= first_seg).astype(jnp.int32)
            for s in range(1, blocks)
        ]
        + picks
    )
    kernel = functools.partial(
        attention_kernel,
        layout=tuple(len(arrays) for arrays, _ in received),
        group_size=group_size,
        head_dim=head_dim,
        score_scale=score_scale,
    )
    width = group_size * head_dim
    grid_spec = pltpu.PrefetchScalarGridSpec(
        num_scalar_prefetch=1,
        grid=(heads_kv,),
        in_specs=[
            pl.BlockSpec((local_rows, width), lambda g, f: (0, g)),
            pl.BlockSpec((local_rows, 1), lambda g, f: (0, 0)),
            pl.BlockSpec((blocks, local_rows), lambda g, f: (0, 0)),
        ]
        + [
            pl.BlockSpec(memory_space=pltpu.VMEM)
            for arrays, _ in received
            for _ in arrays
        ],
        out_specs=pl.BlockSpec((local_rows, width), lambda g, f: (0, g)),
        scratch_shapes=[
            pltpu.VMEM((group_size * local_rows, 128), jnp.float32),
            pltpu.VMEM((group_size * local_rows, 2 * head_dim), jnp.float32),
        ],
    )
    return pl.pallas_call(
        kernel,
        grid_spec=grid_spec,
        out_shape=jax.ShapeDtypeStruct((local_rows, heads * head_dim), jnp.bfloat16),
        compiler_params=pltpu.CompilerParams(dimension_semantics=("arbitrary",)),
        interpret=INTERPRET,
    )(
        flags,
        queries.reshape(local_rows, heads * head_dim),
        seg_local.reshape(local_rows, 1),
        segk,
        *[array for arrays, _ in received for array in arrays],
    )


def make_on_device(help_size):
    partner = [(0, 1), (1, 0)]

    def on_device(queries, keys_values, segment_ids, residual, out_weight):
        local_rows = queries.shape[0]
        width = out_weight.shape[1]
        gathered = lax.all_gather(out_weight, "z", axis=0)
        seg_local = segment_ids.reshape(local_rows)
        helper = lax.axis_index("help")
        core = lax.axis_index("core")
        first = core == 0
        planes = gathered.shape[0]
        stream = residual.reshape(local_rows, planes, 2, width)
        own_cols = jnp.where(first, stream[:, :, 0], stream[:, :, 1])
        other_cols = jnp.where(first, stream[:, :, 1], stream[:, :, 0])
        partner_res = lax.ppermute(other_cols, "core", partner)
        attended = tokens_attention(queries, keys_values, seg_local, helper, help_size)
        partner_att = lax.ppermute(attended, "core", partner)

        def project(rows, res):
            summed = jnp.einsum(
                "qk,zkn->qzn", rows, gathered, preferred_element_type=jnp.float32
            )
            return (res.astype(jnp.float32) + summed).astype(jnp.bfloat16)

        mine = project(attended, own_cols)
        theirs = project(partner_att, partner_res)
        back = lax.ppermute(theirs, "core", partner)
        col0 = jnp.where(first, mine, back)
        col1 = jnp.where(first, back, mine)
        return jnp.stack([col0, col1], axis=2).reshape(local_rows, planes * 2 * width)

    return on_device


def solution(mesh):
    dp_size, help_size = mesh.devices.shape
    split = Mesh(mesh.devices.reshape(dp_size // 2, 2, help_size), ("z", "core", "help"))
    rows = ("z", "core", "help")
    return jax.shard_map(
        make_on_device(help_size),
        mesh=split,
        in_specs=(
            P(rows, None, None),
            P(rows, None, None),
            P(("z", "core"), "help"),
            P(rows, None),
            P(None, ("z", "core")),
        ),
        out_specs=P(rows, None),
        check_vma=False,
    )
```

```python
import functools
import math

import jax
import jax.numpy as jnp
from jax import lax
from jax.experimental import pallas as pl
from jax.experimental.pallas import tpu as pltpu
from jax.sharding import Mesh
from jax.sharding import PartitionSpec as P

masked_score = -1e30
MOST = 2048
SEG_ROWS = 16
INTERPRET = False
QUERY_CHUNK = 128


def attention_kernel(
    flags_ref, q_ref, segq_ref, segk_ref, *refs, layout, group_size, head_dim, score_scale
):
    blocks = len(layout)
    count = 1 + max(i for sources in layout for i in sources)
    kv_refs = [tuple(refs[i] for i in sources) for sources in layout]
    o_ref = refs[count]
    m_ref, acc_ref = refs[count + 1 :]
    rows = q_ref.shape[0]
    chunks = rows // QUERY_CHUNK
    lanes = m_ref.shape[1]
    exp2_scale = score_scale * math.log2(math.e)
    m_ref[...] = jnp.full(m_ref.shape, masked_score, jnp.float32)
    acc_ref[...] = jnp.zeros(acc_ref.shape, jnp.float32)
    ones = jnp.ones((rows, head_dim), jnp.bfloat16)
    head = pl.program_id(0)

    for s in range(blocks):

        def step(s=s):
            if len(kv_refs[s]) == 1:
                kv = kv_refs[s][0][head, :rows, :]
            else:
                first = kv_refs[s][0][head, :rows, :]
                pick = jnp.full(first.shape, flags_ref[blocks + s], jnp.int32)
                kv = jnp.where(pick > 0, first, kv_refs[s][1][head, :rows, :])
            keys = kv[:, :head_dim]
            values = jnp.concatenate([kv[:, head_dim:], ones], axis=1)
            segk = segk_ref[s : s + 1, :]
            for c in range(chunks):
                lo = c * QUERY_CHUNK
                allowed = segq_ref[lo : lo + QUERY_CHUNK, :] == segk
                if s == 0:
                    qi = lax.broadcasted_iota(jnp.int32, (QUERY_CHUNK, rows), 0) + lo
                    ki = lax.broadcasted_iota(jnp.int32, (QUERY_CHUNK, rows), 1)
                    allowed = jnp.logical_and(allowed, ki <= qi)
                bias = jnp.where(allowed, 0.0, masked_score).astype(jnp.float32)
                for h in range(group_size):
                    part = q_ref[lo : lo + QUERY_CHUNK, h * head_dim : (h + 1) * head_dim]
                    scores = (
                        lax.dot_general(
                            part,
                            keys,
                            (((1,), (1,)), ((), ())),
                            preferred_element_type=jnp.float32,
                        )
                        + bias
                    )
                    r = slice(h * rows + lo, h * rows + lo + QUERY_CHUNK)
                    m_old = m_ref[r, :]
                    m_new = jnp.maximum(m_old, jnp.max(scores, axis=1, keepdims=True))
                    wide = jnp.concatenate([m_new] * (rows // lanes), axis=1)
                    weights = jnp.exp2((scores - wide) * exp2_scale)
                    factor = jnp.exp2((m_old - m_new) * exp2_scale)
                    factor = jnp.concatenate([factor] * (2 * head_dim // lanes), axis=1)
                    acc_ref[r, :] = acc_ref[r, :] * factor + jnp.dot(
                        weights.astype(jnp.bfloat16), values, preferred_element_type=jnp.float32
                    )
                    m_ref[r, :] = m_new

        if s == 0:
            step()
        else:
            pl.when(flags_ref[s] > 0)(step)

    for h in range(group_size):
        r = slice(h * rows, (h + 1) * rows)
        acc = acc_ref[r, :]
        o_ref[:, h * head_dim : (h + 1) * head_dim] = (
            acc[:, :head_dim] / acc[:, head_dim:]
        ).astype(o_ref.dtype)


def tokens_attention(queries, keys_values, seg_local, helper, help_size):
    local_rows, heads, head_dim = queries.shape
    heads_kv = keys_values.shape[1]
    group_size = heads // heads_kv
    pair = keys_values.shape[2]
    score_scale = 1.0 / math.sqrt(head_dim)
    flat = jnp.transpose(keys_values, (1, 0, 2))
    seg_row = jnp.zeros((heads_kv, SEG_ROWS, pair), jnp.bfloat16)
    seg_row = seg_row.at[0, 0, :local_rows].set(seg_local.astype(jnp.bfloat16))
    packed = jnp.concatenate([flat, seg_row], axis=1)
    reach = min((MOST - 1 + local_rows - 1) // local_rows, help_size - 1)
    across = math.isqrt(help_size)
    one_back = lax.ppermute(
        packed, "help", [(j, j + across) for j in range(help_size - across)]
    )
    two_back = lax.ppermute(
        packed, "help", [(j, j + 2 * across) for j in range(help_size - 2 * across)]
    )
    column = helper % across
    rows_of = help_size // across
    pieces = {0: ((packed,), True), across: ((one_back,), True), 2 * across: ((two_back,), True)}
    for k in range(1, across):
        ring = lambda xs: [
            (y * across + x, y * across + (x + k) % across) for y in range(rows_of) for x in xs
        ]
        early = lax.ppermute(packed, "help", ring(range(across - k)))
        late_one = lax.ppermute(one_back, "help", ring(range(across)))
        late_two = lax.ppermute(two_back, "help", ring(range(across - k, across)))
        direct = column >= k
        pieces[k] = ((early, late_one), direct)
        pieces[k + across] = ((late_one, late_two), direct)
    received = [pieces[s] for s in range(reach + 1)]
    blocks = len(received)

    def seg_of(piece):
        arrays, direct = piece
        rows = [a[0, local_rows, :local_rows].astype(jnp.int32) for a in arrays]
        return rows[0] if len(rows) == 1 else jnp.where(direct, rows[0], rows[1])

    segk = jnp.stack([seg_local] + [seg_of(p) for p in received[1:]])
    picks = [jnp.asarray(direct, jnp.int32) for _, direct in received]
    operands, layout = [], []
    for arrays, _ in received:
        sources = []
        for array in arrays:
            found = [i for i, known in enumerate(operands) if known is array]
            if not found:
                operands.append(array)
                found = [len(operands) - 1]
            sources.append(found[0])
        layout.append(tuple(sources))
    first_seg = seg_local[0]
    flags = jnp.stack(
        [jnp.int32(1)]
        + [
            jnp.logical_and(helper >= s, segk[s, local_rows - 1] >= first_seg).astype(jnp.int32)
            for s in range(1, blocks)
        ]
        + picks
    )
    kernel = functools.partial(
        attention_kernel,
        layout=tuple(layout),
        group_size=group_size,
        head_dim=head_dim,
        score_scale=score_scale,
    )
    width = group_size * head_dim
    grid_spec = pltpu.PrefetchScalarGridSpec(
        num_scalar_prefetch=1,
        grid=(heads_kv,),
        in_specs=[
            pl.BlockSpec((local_rows, width), lambda g, f: (0, g)),
            pl.BlockSpec((local_rows, 1), lambda g, f: (0, 0)),
            pl.BlockSpec((blocks, local_rows), lambda g, f: (0, 0)),
        ]
        + [pl.BlockSpec(memory_space=pltpu.VMEM) for _ in operands],
        out_specs=pl.BlockSpec((local_rows, width), lambda g, f: (0, g)),
        scratch_shapes=[
            pltpu.VMEM((group_size * local_rows, 128), jnp.float32),
            pltpu.VMEM((group_size * local_rows, 2 * head_dim), jnp.float32),
        ],
    )
    return pl.pallas_call(
        kernel,
        grid_spec=grid_spec,
        out_shape=jax.ShapeDtypeStruct((local_rows, heads * head_dim), jnp.bfloat16),
        compiler_params=pltpu.CompilerParams(dimension_semantics=("arbitrary",)),
        interpret=INTERPRET,
    )(
        flags,
        queries.reshape(local_rows, heads * head_dim),
        seg_local.reshape(local_rows, 1),
        segk,
        *operands,
    )


def make_on_device(help_size):
    partner = [(0, 1), (1, 0)]

    def on_device(queries, keys_values, segment_ids, residual, out_weight):
        local_rows = queries.shape[0]
        width = out_weight.shape[1]
        gathered = lax.all_gather(out_weight, "z", axis=0)
        seg_local = segment_ids.reshape(local_rows)
        helper = lax.axis_index("help")
        core = lax.axis_index("core")
        first = core == 0
        planes = gathered.shape[0]
        stream = residual.reshape(local_rows, planes, 2, width)
        own_cols = jnp.where(first, stream[:, :, 0], stream[:, :, 1])
        other_cols = jnp.where(first, stream[:, :, 1], stream[:, :, 0])
        partner_res = lax.ppermute(other_cols, "core", partner)
        attended = tokens_attention(queries, keys_values, seg_local, helper, help_size)
        partner_att = lax.ppermute(attended, "core", partner)

        def project(rows, res):
            summed = jnp.einsum(
                "qk,zkn->qzn", rows, gathered, preferred_element_type=jnp.float32
            )
            return (res.astype(jnp.float32) + summed).astype(jnp.bfloat16)

        mine = project(attended, own_cols)
        theirs = project(partner_att, partner_res)
        back = lax.ppermute(theirs, "core", partner)
        col0 = jnp.where(first, mine, back)
        col1 = jnp.where(first, back, mine)
        return jnp.stack([col0, col1], axis=2).reshape(local_rows, planes * 2 * width)

    return on_device


def solution(mesh):
    dp_size, help_size = mesh.devices.shape
    split = Mesh(mesh.devices.reshape(dp_size // 2, 2, help_size), ("z", "core", "help"))
    rows = ("z", "core", "help")
    return jax.shard_map(
        make_on_device(help_size),
        mesh=split,
        in_specs=(
            P(rows, None, None),
            P(rows, None, None),
            P(("z", "core"), "help"),
            P(rows, None),
            P(None, ("z", "core")),
        ),
        out_specs=P(rows, None),
        check_vma=False,
    )
```

```python
import functools
import math

import jax
import jax.numpy as jnp
from jax import lax
from jax.experimental import pallas as pl
from jax.experimental.pallas import tpu as pltpu
from jax.sharding import Mesh
from jax.sharding import PartitionSpec as P

masked_score = -1e30
MOST = 2048
SEG_ROWS = 16
INTERPRET = False
QUERY_CHUNK = 128


def attention_kernel(
    flags_ref, q_ref, segq_ref, segk_ref, *refs, layout, group_size, head_dim, score_scale
):
    blocks = len(layout)
    count = 1 + max(i for sources in layout for i in sources)
    kv_refs = [tuple(refs[i] for i in sources) for sources in layout]
    o_ref = refs[count]
    m_ref, acc_ref = refs[count + 1 :]
    rows = q_ref.shape[0]
    chunks = rows // QUERY_CHUNK
    lanes = m_ref.shape[1]
    exp2_scale = score_scale * math.log2(math.e)
    m_ref[...] = jnp.full(m_ref.shape, masked_score, jnp.float32)
    acc_ref[...] = jnp.zeros(acc_ref.shape, jnp.float32)
    ones = jnp.ones((rows, head_dim), jnp.bfloat16)
    head = pl.program_id(0)

    for s in range(blocks):

        def step(s=s):
            if len(kv_refs[s]) == 1:
                kv = kv_refs[s][0][head, :rows, :]
            else:
                first = kv_refs[s][0][head, :rows, :]
                pick = jnp.full(first.shape, flags_ref[blocks + s], jnp.int32)
                kv = jnp.where(pick > 0, first, kv_refs[s][1][head, :rows, :])
            keys = kv[:, :head_dim]
            values = jnp.concatenate([kv[:, head_dim:], ones], axis=1)
            segk = segk_ref[s : s + 1, :]
            for c in range(chunks):
                lo = c * QUERY_CHUNK
                allowed = segq_ref[lo : lo + QUERY_CHUNK, :] == segk
                if s == 0:
                    qi = lax.broadcasted_iota(jnp.int32, (QUERY_CHUNK, rows), 0) + lo
                    ki = lax.broadcasted_iota(jnp.int32, (QUERY_CHUNK, rows), 1)
                    allowed = jnp.logical_and(allowed, ki <= qi)
                bias = jnp.where(allowed, 0.0, masked_score).astype(jnp.float32)
                for h in range(group_size):
                    part = q_ref[lo : lo + QUERY_CHUNK, h * head_dim : (h + 1) * head_dim]
                    scores = (
                        lax.dot_general(
                            part,
                            keys,
                            (((1,), (1,)), ((), ())),
                            preferred_element_type=jnp.float32,
                        )
                        + bias
                    )
                    r = slice(h * rows + lo, h * rows + lo + QUERY_CHUNK)
                    m_old = m_ref[r, :]
                    m_new = jnp.maximum(m_old, jnp.max(scores, axis=1, keepdims=True))
                    wide = jnp.concatenate([m_new] * (rows // lanes), axis=1)
                    weights = jnp.exp2((scores - wide) * exp2_scale)
                    factor = jnp.exp2((m_old - m_new) * exp2_scale)
                    factor = jnp.concatenate([factor] * (2 * head_dim // lanes), axis=1)
                    acc_ref[r, :] = acc_ref[r, :] * factor + jnp.dot(
                        weights.astype(jnp.bfloat16), values, preferred_element_type=jnp.float32
                    )
                    m_ref[r, :] = m_new

        if s == 0:
            step()
        else:
            pl.when(flags_ref[s] > 0)(step)

    for h in range(group_size):
        r = slice(h * rows, (h + 1) * rows)
        acc = acc_ref[r, :]
        o_ref[:, h * head_dim : (h + 1) * head_dim] = (
            acc[:, :head_dim] / acc[:, head_dim:]
        ).astype(o_ref.dtype)


def tokens_attention(queries, keys_values, seg_local, helper, help_size):
    local_rows, heads, head_dim = queries.shape
    heads_kv = keys_values.shape[1]
    group_size = heads // heads_kv
    pair = keys_values.shape[2]
    score_scale = 1.0 / math.sqrt(head_dim)
    flat = jnp.transpose(keys_values, (1, 0, 2))
    seg_row = jnp.zeros((heads_kv, SEG_ROWS, pair), jnp.bfloat16)
    seg_row = seg_row.at[0, 0, :local_rows].set(seg_local.astype(jnp.bfloat16))
    packed = jnp.concatenate([flat, seg_row], axis=1)
    reach = min((MOST - 1 + local_rows - 1) // local_rows, help_size - 1)
    across = math.isqrt(help_size)
    one_back = lax.ppermute(
        packed, "help", [(j, j + across) for j in range(help_size - across)]
    )
    two_back = lax.ppermute(
        packed, "help", [(j, j + 2 * across) for j in range(help_size - 2 * across)]
    )
    column = helper % across
    rows_of = help_size // across
    pieces = {0: ((packed,), True), across: ((one_back,), True), 2 * across: ((two_back,), True)}
    for k in range(1, across):
        ring = lambda xs: [
            (y * across + x, y * across + (x + k) % across) for y in range(rows_of) for x in xs
        ]
        early = lax.ppermute(packed, "help", ring(range(across - k)))
        late_one = lax.ppermute(one_back, "help", ring(range(across)))
        late_two = lax.ppermute(two_back, "help", ring(range(across - k, across)))
        direct = column >= k
        pieces[k] = ((early, late_one), direct)
        pieces[k + across] = ((late_one, late_two), direct)
    received = [pieces[s] for s in range(reach + 1)]
    blocks = len(received)

    def seg_of(piece):
        arrays, direct = piece
        rows = [a[0, local_rows, :local_rows].astype(jnp.int32) for a in arrays]
        return rows[0] if len(rows) == 1 else jnp.where(direct, rows[0], rows[1])

    segk = jnp.stack([seg_local] + [seg_of(p) for p in received[1:]])
    picks = [jnp.asarray(direct, jnp.int32) for _, direct in received]
    operands, layout = [], []
    for arrays, _ in received:
        sources = []
        for array in arrays:
            found = [i for i, known in enumerate(operands) if known is array]
            if not found:
                operands.append(array)
                found = [len(operands) - 1]
            sources.append(found[0])
        layout.append(tuple(sources))
    first_seg = seg_local[0]
    flags = jnp.stack(
        [jnp.int32(1)]
        + [
            jnp.logical_and(helper >= s, segk[s, local_rows - 1] >= first_seg).astype(jnp.int32)
            for s in range(1, blocks)
        ]
        + picks
    )
    kernel = functools.partial(
        attention_kernel,
        layout=tuple(layout),
        group_size=group_size,
        head_dim=head_dim,
        score_scale=score_scale,
    )
    width = group_size * head_dim
    grid_spec = pltpu.PrefetchScalarGridSpec(
        num_scalar_prefetch=1,
        grid=(heads_kv,),
        in_specs=[
            pl.BlockSpec((local_rows, width), lambda g, f: (0, g)),
            pl.BlockSpec((local_rows, 1), lambda g, f: (0, 0)),
            pl.BlockSpec((blocks, local_rows), lambda g, f: (0, 0)),
        ]
        + [pl.BlockSpec(memory_space=pltpu.VMEM) for _ in operands],
        out_specs=pl.BlockSpec((local_rows, width), lambda g, f: (0, g)),
        scratch_shapes=[
            pltpu.VMEM((group_size * local_rows, 128), jnp.float32),
            pltpu.VMEM((group_size * local_rows, 2 * head_dim), jnp.float32),
        ],
    )
    return pl.pallas_call(
        kernel,
        grid_spec=grid_spec,
        out_shape=jax.ShapeDtypeStruct((local_rows, heads * head_dim), jnp.bfloat16),
        compiler_params=pltpu.CompilerParams(dimension_semantics=("arbitrary",)),
        interpret=INTERPRET,
    )(
        flags,
        queries.reshape(local_rows, heads * head_dim),
        seg_local.reshape(local_rows, 1),
        segk,
        *operands,
    )


def make_on_device(help_size):
    def on_device(queries, keys_values, segment_ids, residual, out_weight):
        local_rows = queries.shape[0]
        width = out_weight.shape[1]
        gathered = lax.all_gather(out_weight, "z", axis=0)
        seg_local = segment_ids.reshape(local_rows)
        helper = lax.axis_index("help")
        planes = gathered.shape[0]
        stream = residual.reshape(local_rows, planes, 2, width)
        full = lax.all_gather(gathered, "core", axis=0)
        attended = tokens_attention(queries, keys_values, seg_local, helper, help_size)
        summed = jnp.einsum("qk,czkn->qzcn", attended, full, preferred_element_type=jnp.float32)
        joined = (stream.astype(jnp.float32) + summed).astype(jnp.bfloat16)
        return joined.reshape(local_rows, planes * 2 * width)

    return on_device


def solution(mesh):
    dp_size, help_size = mesh.devices.shape
    split = Mesh(mesh.devices.reshape(dp_size // 2, 2, help_size), ("z", "core", "help"))
    rows = ("z", "core", "help")
    return jax.shard_map(
        make_on_device(help_size),
        mesh=split,
        in_specs=(
            P(rows, None, None),
            P(rows, None, None),
            P(("z", "core"), "help"),
            P(rows, None),
            P(None, ("z", "core")),
        ),
        out_specs=P(rows, None),
        check_vma=False,
    )
```

```python
import functools
import math

import jax
import jax.numpy as jnp
from jax import lax
from jax.experimental import pallas as pl
from jax.experimental.pallas import tpu as pltpu
from jax.sharding import Mesh
from jax.sharding import PartitionSpec as P

masked_score = -1e30
MOST = 2048
INTERPRET = False
QUERY_CHUNK = 128


def attention_kernel(
    flags_ref, q_ref, segq_ref, segk_ref, *refs, blocks, group_size, head_dim, score_scale
):
    kv_refs = refs[:blocks]
    o_ref = refs[blocks]
    m_ref, acc_ref = refs[blocks + 1 :]
    rows = q_ref.shape[0]
    chunks = rows // QUERY_CHUNK
    lanes = m_ref.shape[1]
    exp2_scale = score_scale * math.log2(math.e)
    m_ref[...] = jnp.full(m_ref.shape, masked_score, jnp.float32)
    acc_ref[...] = jnp.zeros(acc_ref.shape, jnp.float32)
    ones = jnp.ones((rows, head_dim), jnp.bfloat16)

    for s in range(blocks):

        def step(s=s):
            keys = kv_refs[s][:, :head_dim]
            values = jnp.concatenate([kv_refs[s][:, head_dim:], ones], axis=1)
            segk = segk_ref[s : s + 1, :]
            for c in range(chunks):
                lo = c * QUERY_CHUNK
                allowed = segq_ref[lo : lo + QUERY_CHUNK, :] == segk
                if s == 0:
                    qi = lax.broadcasted_iota(jnp.int32, (QUERY_CHUNK, rows), 0) + lo
                    ki = lax.broadcasted_iota(jnp.int32, (QUERY_CHUNK, rows), 1)
                    allowed = jnp.logical_and(allowed, ki <= qi)
                bias = jnp.where(allowed, 0.0, masked_score).astype(jnp.float32)
                for h in range(group_size):
                    part = q_ref[lo : lo + QUERY_CHUNK, h * head_dim : (h + 1) * head_dim]
                    scores = (
                        lax.dot_general(
                            part,
                            keys,
                            (((1,), (1,)), ((), ())),
                            preferred_element_type=jnp.float32,
                        )
                        + bias
                    )
                    r = slice(h * rows + lo, h * rows + lo + QUERY_CHUNK)
                    m_old = m_ref[r, :]
                    m_new = jnp.maximum(m_old, jnp.max(scores, axis=1, keepdims=True))
                    wide = jnp.concatenate([m_new] * (rows // lanes), axis=1)
                    weights = jnp.exp2((scores - wide) * exp2_scale)
                    factor = jnp.exp2((m_old - m_new) * exp2_scale)
                    factor = jnp.concatenate([factor] * (2 * head_dim // lanes), axis=1)
                    acc_ref[r, :] = acc_ref[r, :] * factor + jnp.dot(
                        weights.astype(jnp.bfloat16), values, preferred_element_type=jnp.float32
                    )
                    m_ref[r, :] = m_new

        if s == 0:
            step()
        else:
            pl.when(flags_ref[s] > 0)(step)

    for h in range(group_size):
        r = slice(h * rows, (h + 1) * rows)
        acc = acc_ref[r, :]
        o_ref[:, h * head_dim : (h + 1) * head_dim] = (
            acc[:, :head_dim] / acc[:, head_dim:]
        ).astype(o_ref.dtype)


def tokens_attention(queries, keys_values, seg_local, helper, help_size):
    local_rows, heads, head_dim = queries.shape
    heads_kv = keys_values.shape[1]
    group_size = heads // heads_kv
    pair = keys_values.shape[2]
    score_scale = 1.0 / math.sqrt(head_dim)
    packed = keys_values.reshape(local_rows, heads_kv * pair)
    row_segs = lax.all_gather(seg_local, "help", axis=0)
    reach = min((MOST - 1 + local_rows - 1) // local_rows, help_size - 1)
    across = math.isqrt(help_size)
    one_back = lax.ppermute(
        packed, "help", [(j, j + across) for j in range(help_size - across)]
    )
    two_back = lax.ppermute(
        packed, "help", [(j, j + 2 * across) for j in range(help_size - 2 * across)]
    )
    column = helper % across
    rows_of = help_size // across
    pieces = {0: (packed, None), across: (one_back, None), 2 * across: (two_back, None)}
    for k in range(1, across):
        ring = lambda xs: [
            (y * across + x, y * across + (x + k) % across) for y in range(rows_of) for x in xs
        ]
        early = lax.ppermute(packed, "help", ring(range(across - k)))
        late_one = lax.ppermute(one_back, "help", ring(range(across)))
        late_two = lax.ppermute(two_back, "help", ring(range(across - k, across)))
        direct = column >= k
        pieces[k] = (jnp.where(direct, early, late_one), None)
        pieces[k + across] = (jnp.where(direct, late_one, late_two), None)
    received = [pieces[s] for s in range(reach + 1)]
    blocks = len(received)

    segk = jnp.stack(
        [seg_local]
        + [
            lax.dynamic_index_in_dim(row_segs, jnp.maximum(helper - s, 0), keepdims=False)
            for s in range(1, blocks)
        ]
    )
    first_seg = seg_local[0]
    flags = jnp.stack(
        [jnp.int32(1)]
        + [
            jnp.logical_and(helper >= s, segk[s, local_rows - 1] >= first_seg).astype(jnp.int32)
            for s in range(1, blocks)
        ]
    )
    kernel = functools.partial(
        attention_kernel,
        blocks=blocks,
        group_size=group_size,
        head_dim=head_dim,
        score_scale=score_scale,
    )
    width = group_size * head_dim
    grid_spec = pltpu.PrefetchScalarGridSpec(
        num_scalar_prefetch=1,
        grid=(heads_kv,),
        in_specs=[
            pl.BlockSpec((local_rows, width), lambda g, f: (0, g)),
            pl.BlockSpec((local_rows, 1), lambda g, f: (0, 0)),
            pl.BlockSpec((blocks, local_rows), lambda g, f: (0, 0)),
        ]
        + [
            pl.BlockSpec((local_rows, pair), lambda g, f: (0, g))
            if index is None
            else pl.BlockSpec((None, local_rows, pair), lambda g, f, i=index: (i, 0, g))
            for _, index in received
        ],
        out_specs=pl.BlockSpec((local_rows, width), lambda g, f: (0, g)),
        scratch_shapes=[
            pltpu.VMEM((group_size * local_rows, 128), jnp.float32),
            pltpu.VMEM((group_size * local_rows, 2 * head_dim), jnp.float32),
        ],
    )
    return pl.pallas_call(
        kernel,
        grid_spec=grid_spec,
        out_shape=jax.ShapeDtypeStruct((local_rows, heads * head_dim), jnp.bfloat16),
        compiler_params=pltpu.CompilerParams(dimension_semantics=("arbitrary",)),
        interpret=INTERPRET,
    )(
        flags,
        queries.reshape(local_rows, heads * head_dim),
        seg_local.reshape(local_rows, 1),
        segk,
        *[array for array, _ in received],
    )


def make_on_device(help_size):
    partner = [(0, 1), (1, 0)]

    def on_device(queries, keys_values, segment_ids, residual, out_weight):
        local_rows = queries.shape[0]
        width = out_weight.shape[1]
        gathered = lax.all_gather(out_weight, "z", axis=0)
        seg_local = segment_ids.reshape(local_rows)
        helper = lax.axis_index("help")
        core = lax.axis_index("core")
        first = core == 0
        planes = gathered.shape[0]
        stream = residual.reshape(local_rows, planes, 2, width)
        own_cols = jnp.where(first, stream[:, :, 0], stream[:, :, 1])
        other_cols = jnp.where(first, stream[:, :, 1], stream[:, :, 0])
        partner_res = lax.ppermute(other_cols, "core", partner)
        attended = tokens_attention(queries, keys_values, seg_local, helper, help_size)
        partner_att = lax.ppermute(attended, "core", partner)

        def project(rows, res):
            summed = jnp.einsum(
                "qk,zkn->qzn", rows, gathered, preferred_element_type=jnp.float32
            )
            return (res.astype(jnp.float32) + summed).astype(jnp.bfloat16)

        mine = project(attended, own_cols)
        theirs = project(partner_att, partner_res)
        back = lax.ppermute(theirs, "core", partner)
        col0 = jnp.where(first, mine, back)
        col1 = jnp.where(first, back, mine)
        return jnp.stack([col0, col1], axis=2).reshape(local_rows, planes * 2 * width)

    return on_device


def solution(mesh):
    dp_size, help_size = mesh.devices.shape
    split = Mesh(mesh.devices.reshape(dp_size // 2, 2, help_size), ("z", "core", "help"))
    rows = ("z", "core", "help")
    return jax.shard_map(
        make_on_device(help_size),
        mesh=split,
        in_specs=(
            P(rows, None, None),
            P(rows, None, None),
            P(("z", "core"), "help"),
            P(rows, None),
            P(None, ("z", "core")),
        ),
        out_specs=P(rows, None),
        check_vma=False,
    )
```

```python
import functools
import math

import jax
import jax.numpy as jnp
from jax import lax
from jax.experimental import pallas as pl
from jax.experimental.pallas import tpu as pltpu
from jax.sharding import Mesh
from jax.sharding import PartitionSpec as P

masked_score = -1e30
MOST = 2048
SEG_ROWS = 16
INTERPRET = False
QUERY_CHUNK = 128


def attention_kernel(
    flags_ref, q_ref, segq_ref, segk_ref, *refs, blocks, group_size, head_dim, score_scale
):
    kv_refs = refs[:blocks]
    o_ref = refs[blocks]
    m_ref, acc_ref = refs[blocks + 1 :]
    rows = q_ref.shape[0]
    chunks = rows // QUERY_CHUNK
    lanes = m_ref.shape[1]
    exp2_scale = score_scale * math.log2(math.e)
    m_ref[...] = jnp.full(m_ref.shape, masked_score, jnp.float32)
    acc_ref[...] = jnp.zeros(acc_ref.shape, jnp.float32)
    ones = jnp.ones((rows, head_dim), jnp.bfloat16)

    for s in range(blocks):

        def step(s=s):
            keys = kv_refs[s][:, :head_dim]
            values = jnp.concatenate([kv_refs[s][:, head_dim:], ones], axis=1)
            segk = segk_ref[s : s + 1, :]
            for c in range(chunks):
                lo = c * QUERY_CHUNK
                allowed = segq_ref[lo : lo + QUERY_CHUNK, :] == segk
                if s == 0:
                    qi = lax.broadcasted_iota(jnp.int32, (QUERY_CHUNK, rows), 0) + lo
                    ki = lax.broadcasted_iota(jnp.int32, (QUERY_CHUNK, rows), 1)
                    allowed = jnp.logical_and(allowed, ki <= qi)
                bias = jnp.where(allowed, 0.0, masked_score).astype(jnp.float32)
                for h in range(group_size):
                    part = q_ref[lo : lo + QUERY_CHUNK, h * head_dim : (h + 1) * head_dim]
                    scores = (
                        lax.dot_general(
                            part,
                            keys,
                            (((1,), (1,)), ((), ())),
                            preferred_element_type=jnp.float32,
                        )
                        + bias
                    )
                    r = slice(h * rows + lo, h * rows + lo + QUERY_CHUNK)
                    m_old = m_ref[r, :]
                    m_new = jnp.maximum(m_old, jnp.max(scores, axis=1, keepdims=True))
                    wide = jnp.concatenate([m_new] * (rows // lanes), axis=1)
                    weights = jnp.exp2((scores - wide) * exp2_scale)
                    factor = jnp.exp2((m_old - m_new) * exp2_scale)
                    factor = jnp.concatenate([factor] * (2 * head_dim // lanes), axis=1)
                    acc_ref[r, :] = acc_ref[r, :] * factor + jnp.dot(
                        weights.astype(jnp.bfloat16), values, preferred_element_type=jnp.float32
                    )
                    m_ref[r, :] = m_new

        if s == 0:
            step()
        else:
            pl.when(flags_ref[s] > 0)(step)

    for h in range(group_size):
        r = slice(h * rows, (h + 1) * rows)
        acc = acc_ref[r, :]
        o_ref[:, h * head_dim : (h + 1) * head_dim] = (
            acc[:, :head_dim] / acc[:, head_dim:]
        ).astype(o_ref.dtype)


def tokens_attention(queries, keys_values, seg_local, helper, help_size):
    local_rows, heads, head_dim = queries.shape
    heads_kv = keys_values.shape[1]
    group_size = heads // heads_kv
    pair = keys_values.shape[2]
    score_scale = 1.0 / math.sqrt(head_dim)
    flat = keys_values.reshape(local_rows, heads_kv * pair)
    seg_row = jnp.zeros((SEG_ROWS, heads_kv * pair), jnp.bfloat16)
    seg_row = seg_row.at[0, :local_rows].set(seg_local.astype(jnp.bfloat16))
    packed = jnp.concatenate([flat, seg_row], axis=0)
    reach = min((MOST - 1 + local_rows - 1) // local_rows, help_size - 1)
    across = math.isqrt(help_size)
    one_back = lax.ppermute(
        packed, "help", [(j, j + across) for j in range(help_size - across)]
    )
    two_back = lax.ppermute(
        one_back, "help", [(j, j + across) for j in range(help_size - across)]
    )
    column = helper % across
    rows_of = help_size // across
    pieces = {0: (packed, None), across: (one_back, None), 2 * across: (two_back, None)}
    for k in range(1, across):
        ring = lambda xs: [
            (y * across + x, y * across + (x + k) % across) for y in range(rows_of) for x in xs
        ]
        early = lax.ppermute(packed, "help", ring(range(across - k)))
        late_one = lax.ppermute(one_back, "help", ring(range(across)))
        late_two = lax.ppermute(two_back, "help", ring(range(across - k, across)))
        direct = column >= k
        pieces[k] = (jnp.where(direct, early, late_one), None)
        pieces[k + across] = (jnp.where(direct, late_one, late_two), None)
    received = [pieces[s] for s in range(reach + 1)]
    blocks = len(received)

    def seg_of(piece):
        array, index = piece
        row = array[local_rows] if index is None else array[index, local_rows]
        return row[:local_rows].astype(jnp.int32)

    segk = jnp.stack([seg_local] + [seg_of(p) for p in received[1:]])
    first_seg = seg_local[0]
    flags = jnp.stack(
        [jnp.int32(1)]
        + [
            jnp.logical_and(helper >= s, segk[s, local_rows - 1] >= first_seg).astype(jnp.int32)
            for s in range(1, blocks)
        ]
    )
    kernel = functools.partial(
        attention_kernel,
        blocks=blocks,
        group_size=group_size,
        head_dim=head_dim,
        score_scale=score_scale,
    )
    width = group_size * head_dim
    grid_spec = pltpu.PrefetchScalarGridSpec(
        num_scalar_prefetch=1,
        grid=(heads_kv,),
        in_specs=[
            pl.BlockSpec((local_rows, width), lambda g, f: (0, g)),
            pl.BlockSpec((local_rows, 1), lambda g, f: (0, 0)),
            pl.BlockSpec((blocks, local_rows), lambda g, f: (0, 0)),
        ]
        + [
            pl.BlockSpec((local_rows, pair), lambda g, f: (0, g))
            if index is None
            else pl.BlockSpec((None, local_rows, pair), lambda g, f, i=index: (i, 0, g))
            for _, index in received
        ],
        out_specs=pl.BlockSpec((local_rows, width), lambda g, f: (0, g)),
        scratch_shapes=[
            pltpu.VMEM((group_size * local_rows, 128), jnp.float32),
            pltpu.VMEM((group_size * local_rows, 2 * head_dim), jnp.float32),
        ],
    )
    return pl.pallas_call(
        kernel,
        grid_spec=grid_spec,
        out_shape=jax.ShapeDtypeStruct((local_rows, heads * head_dim), jnp.bfloat16),
        compiler_params=pltpu.CompilerParams(dimension_semantics=("arbitrary",)),
        interpret=INTERPRET,
    )(
        flags,
        queries.reshape(local_rows, heads * head_dim),
        seg_local.reshape(local_rows, 1),
        segk,
        *[array for array, _ in received],
    )


def make_on_device(help_size):
    partner = [(0, 1), (1, 0)]

    def on_device(queries, keys_values, segment_ids, residual, out_weight):
        local_rows = queries.shape[0]
        width = out_weight.shape[1]
        gathered = lax.all_gather(out_weight, "z", axis=0)
        seg_local = segment_ids.reshape(local_rows)
        helper = lax.axis_index("help")
        core = lax.axis_index("core")
        first = core == 0
        planes = gathered.shape[0]
        stream = residual.reshape(local_rows, planes, 2, width)
        own_cols = jnp.where(first, stream[:, :, 0], stream[:, :, 1])
        other_cols = jnp.where(first, stream[:, :, 1], stream[:, :, 0])
        partner_res = lax.ppermute(other_cols, "core", partner)
        attended = tokens_attention(queries, keys_values, seg_local, helper, help_size)
        partner_att = lax.ppermute(attended, "core", partner)

        def project(rows, res):
            summed = jnp.einsum(
                "qk,zkn->qzn", rows, gathered, preferred_element_type=jnp.float32
            )
            return (res.astype(jnp.float32) + summed).astype(jnp.bfloat16)

        mine = project(attended, own_cols)
        theirs = project(partner_att, partner_res)
        back = lax.ppermute(theirs, "core", partner)
        col0 = jnp.where(first, mine, back)
        col1 = jnp.where(first, back, mine)
        return jnp.stack([col0, col1], axis=2).reshape(local_rows, planes * 2 * width)

    return on_device


def solution(mesh):
    dp_size, help_size = mesh.devices.shape
    split = Mesh(mesh.devices.reshape(dp_size // 2, 2, help_size), ("z", "core", "help"))
    rows = ("z", "core", "help")
    return jax.shard_map(
        make_on_device(help_size),
        mesh=split,
        in_specs=(
            P(rows, None, None),
            P(rows, None, None),
            P(("z", "core"), "help"),
            P(rows, None),
            P(None, ("z", "core")),
        ),
        out_specs=P(rows, None),
        check_vma=False,
    )
```
